32 devices in a mesh: grp: 2 (over x), tile: 16 (over z, y, core).
Axes of the slice: x: 2, y: 2, z: 4, core: 2. Of those that a mesh axis runs over, the one named last changes fastest.
Arguments:
- latent: float32 [32, 1024, 128], P(None, ('grp', 'tile')), parts along dimension 1, may hold values from -6 to 6
- observed: float32 [32, 1024, 128], P(None, ('grp', 'tile')), parts along dimension 1, may hold values from -6 to 6
- noise: float32 [32, 1024, 128], P(None, ('grp', 'tile')), parts along dimension 1, may hold values from -6 to 6
- cloudy: int32 [128], P(('grp', 'tile')), parts along dimension 0, may hold values from 0 to 1, as said below
- timestep: int32 [2], P('grp'), parts along dimension 0, may hold values from 200 to 800
- pos_embed: bfloat16 [256, 2048], replicated, may hold values from -3 to 3
- embed_w: bfloat16 [128, 2048], replicated, may hold values from -0.5 to 0.5
- mod_w: bfloat16 [256, 6144], P(None, 'tile'), may hold values from -0.375 to 0.375
- wq: bfloat16 [2048, 1024], P('tile')
- wk: bfloat16 [2048, 1024], P('tile')
- wv: bfloat16 [2048, 1024], P('tile'), may hold values from -0.125 to 0.125
- wo: bfloat16 [1024, 2048], P(None, 'tile'), may hold values from -0.1875 to 0.1875
- q_gain: float32 [128], replicated, may hold values from 0.6 to 4.2
- k_gain: float32 [128], replicated, may hold values from 0.6 to 4.2
- out_w: bfloat16 [2048, 128], replicated, may hold values from -0.125 to 0.125
- conv_w: float32 [9, 32, 32], replicated, may hold values from -0.375 to 0.375
Outputs:
- estimate: float32 [32, 1024, 128], P(None, ('grp', 'tile')), parts along dimension 1
- next_latent: float32 [32, 1024, 128], P(None, ('grp', 'tile')), parts along dimension 1
The draws below stay inside these ranges and needn't reach their ends.
There are 2 independent parts, one for each index of `grp`. The reference program is written for one: setup_inputs(seed, part) draws one part's arguments, and reference() takes and returns one part's arrays. A program takes and returns all parts, laid end to end along the dimension named above; an argument that names none is the same for every part. Nothing has to cross between parts.
Inputs may be any that keep to these rules, and one draw needn't show every extreme that they name: Exactly 16 tiles of a part are cloudy; each band of 4 tiles holds at most 3 of them, and some band holds exactly 3.
All inputs are finite; a program needn't handle non-finite values.
Results may differ from the reference program's by a relative error of at most 0.0033.
Values may be sent and summed in bfloat16 or wider, within the bound.
No kernel may reach another device: no remote copies, remote signals or barrier semaphores. Data moves between devices by JAX's collectives and lax.ppermute only.
A program may use at most 128 MiB of HBM per device.

```python
import math
import jax
import jax.numpy as jnp
from jax import lax

D = 2048
HD = 128
INNER = 1024
FREQ = 256
LATC = 32
PATCH = 2
PV = 128
TSIDE = 16
TT = 256
TPX = 32
TILES_DEV = 4
TSTEPS = 1000
STRIDE = 20
OWNERS = 16
TILES = 64
HL = 512
WL = 128
N_TILE = 16


def draw_cloudy(key, part):
    owners = TILES // TILES_DEV
    groups = owners // 4
    patterns = jnp.array([[3, 1, 0, 0], [2, 1, 1, 0], [2, 2, 0, 0], [1, 1, 1, 1]], jnp.int32)
    picks = jax.random.randint(jax.random.fold_in(key, 1), (groups,), 0, 4)
    picks = picks.at[0].set(0)
    group_counts = patterns[picks]
    scores = jax.random.randint(jax.random.fold_in(key, 2), (groups, 4), 0, 1 << 20) * 4 + jnp.arange(4, dtype=jnp.int32)[None, :]
    order = jnp.argsort(scores, axis=1)
    group_counts = jnp.take_along_axis(group_counts, order, axis=1)
    counts = jax.random.permutation(jax.random.fold_in(key, 3), group_counts.reshape(owners))
    tile_scores = jax.random.randint(jax.random.fold_in(key, 4), (owners, TILES_DEV), 0, 1 << 20) * TILES_DEV + jnp.arange(TILES_DEV, dtype=jnp.int32)[None, :]
    ranks = jnp.argsort(jnp.argsort(tile_scores, axis=1), axis=1)
    flags = (ranks < counts[:, None]).astype(jnp.int32)
    return flags.reshape(TILES)


def query_key_pair(key):
    first = jax.random.normal(jax.random.fold_in(key, 101), (D, INNER), jnp.float32)
    other = jax.random.normal(jax.random.fold_in(key, 102), (D, INNER), jnp.float32)
    first = jnp.clip(first, -5.0, 5.0)
    other = jnp.clip(other, -5.0, 5.0)
    second = other
    return (first * D ** (-0.5), second * D ** (-0.5))


def draw_wq(key, part):
    return query_key_pair(key)[0].astype(jnp.bfloat16)


def draw_wk(key, part):
    return query_key_pair(key)[1].astype(jnp.bfloat16)


def gain_values(key, salt):
    inner_key = jax.random.fold_in(key, salt)
    values = jax.random.uniform(inner_key, (HD,), jnp.float32, 0.6, 1.8)
    return values


def draw_q_gain(key, part):
    return gain_values(key, 201)


def draw_k_gain(key, part):
    return gain_values(key, 202)


def levels(own_key, shape, cuts, low, high):
    factor_of = 1.0
    for position, blocks in cuts:
        heights = jax.random.uniform(jax.random.fold_in(jax.random.fold_in(own_key, 6), position), (blocks,), jnp.float32, low / len(cuts), high / len(cuts))
        factor_of = factor_of * jnp.repeat(jnp.exp(heights), shape[position] // blocks).reshape((-1,) + (1,) * (len(shape) - 1 - position))
    return factor_of


def normal_values(rng, shape, deviation, most, shards=(), kind=jnp.bfloat16):
    drawn = deviation * jax.random.normal(rng, shape, jnp.float32)
    if shards:
        drawn = drawn * levels(rng, shape, shards, -0.22, 0.18)
    return jnp.clip(drawn, -most, most).astype(kind)


def setup_inputs(seed: int = 0, part: int = 0) -> dict:
    keys = jax.random.split(jax.random.key(seed), 17)
    part_keys = jax.random.split(jax.random.fold_in(keys[16], part), 17)
    latent = normal_values(part_keys[0], (LATC, HL, WL), 1.0, 6.0, ((1, 16),), jnp.float32)
    observed = normal_values(part_keys[1], (LATC, HL, WL), 1.0, 6.0, ((1, 16),), jnp.float32)
    noise = normal_values(part_keys[2], (LATC, HL, WL), 1.0, 6.0, ((1, 16),), jnp.float32)
    cloudy = draw_cloudy(jax.random.fold_in(jax.random.fold_in(keys[16], part), 71), part)
    timestep = jax.random.randint(part_keys[4], (1,), 200, 801).astype(jnp.int32)
    pos_embed = normal_values(keys[5], (TT, D), 0.5, 3.0)
    embed_w = normal_values(keys[6], (PV, D), PV ** -0.5, 0.5)
    mod_w = normal_values(keys[7], (FREQ, 3 * D), FREQ ** -0.5, 0.375, ((1, 16),))
    wq = draw_wq(jax.random.fold_in(keys[16], 71), part)
    wk = draw_wk(jax.random.fold_in(keys[16], 71), part)
    wv = normal_values(keys[10], (D, INNER), D ** -0.5, 0.125, ((0, 16),))
    wo = normal_values(keys[11], (INNER, D), INNER ** -0.5, 0.1875, ((1, 16),))
    q_gain = draw_q_gain(jax.random.fold_in(keys[16], 71), part)
    k_gain = draw_k_gain(jax.random.fold_in(keys[16], 71), part)
    out_w = normal_values(keys[14], (D, PV), D ** -0.5, 0.125)
    conv_w = normal_values(keys[15], (9, LATC, LATC), (9 * LATC) ** -0.5, 0.375, (), jnp.float32)
    return dict(latent=latent, observed=observed, noise=noise, cloudy=cloudy, timestep=timestep, pos_embed=pos_embed, embed_w=embed_w, mod_w=mod_w, wq=wq, wk=wk, wv=wv, wo=wo, q_gain=q_gain, k_gain=k_gain, out_w=out_w, conv_w=conv_w)


def plan(step):
    theta = (step / TSTEPS + 0.008) / 1.008 * (math.pi / 2)
    return (jnp.cos(theta), jnp.sin(theta))

def time_features(step, width):
    half = width // 2
    freqs = jnp.exp(-math.log(10000.0) * jnp.arange(half, dtype=jnp.float32) / half)
    angles = step * freqs
    code = jnp.concatenate([jnp.cos(angles), jnp.sin(angles)])[None, :]
    return jax.nn.silu(code).astype(jnp.bfloat16)

def layer_norm(values):
    center = values - lax.optimization_barrier(jnp.mean(values, axis=-1, keepdims=True))
    spread = lax.optimization_barrier(jnp.mean(center * center, axis=-1, keepdims=True))
    return center * lax.rsqrt(spread + 1e-06)

def head_norm(proj, gain, count):
    shaped = proj.reshape(count, TT, -1, HD)
    scaled = shaped * lax.rsqrt(lax.optimization_barrier(jnp.mean(shaped * shaped, axis=-1, keepdims=True)) + 1e-06)
    return (scaled * gain).astype(jnp.bfloat16)

def denoise_tiles(chosen, embed_w, pos_embed, shift_vec, scale_vec, gate_vec, wq, wk, wv, wo, q_gain, k_gain, out_w):
    count = chosen.shape[0]
    row_count = count * TT
    flat = chosen.reshape(row_count, PV)
    hidden0 = jnp.dot(flat, embed_w, preferred_element_type=jnp.float32).reshape(count, TT, D)
    hidden0 = (hidden0 + pos_embed.astype(jnp.float32)[None]).reshape(row_count, D)
    modulated = (layer_norm(hidden0) * (1.0 + scale_vec) + shift_vec).astype(jnp.bfloat16)
    query_all = jnp.dot(modulated, wq, preferred_element_type=jnp.float32)
    key_all = jnp.dot(modulated, wk, preferred_element_type=jnp.float32)
    value_all = jnp.dot(modulated, wv, preferred_element_type=jnp.float32)
    query_norm = head_norm(query_all, q_gain, count).astype(jnp.float32)
    key_norm = head_norm(key_all, k_gain, count).astype(jnp.float32)
    value_half = value_all.reshape(count, TT, -1, HD).astype(jnp.bfloat16).astype(jnp.float32)
    scores = jnp.einsum('nqhd,nkhd->nhqk', query_norm, key_norm) * HD ** (-0.5)
    peak = lax.optimization_barrier(jnp.max(scores, axis=-1, keepdims=True))
    expo = jnp.exp(scores - peak)
    probs = (expo / lax.optimization_barrier(jnp.sum(expo, axis=-1, keepdims=True))).astype(jnp.bfloat16).astype(jnp.float32)
    mixed = jnp.einsum('nhqk,nkhd->nqhd', probs, value_half).astype(jnp.bfloat16).reshape(row_count, -1)
    attn_out = jnp.dot(mixed, wo, preferred_element_type=jnp.float32)
    hidden1 = hidden0 + gate_vec * attn_out
    final = layer_norm(hidden1).astype(jnp.bfloat16)
    eps_pred = jnp.dot(final, out_w, preferred_element_type=jnp.float32).astype(jnp.bfloat16)
    return eps_pred.reshape(count, TT, PV)

def all_tiles(scene_field):
    shaped = scene_field.reshape(LATC, N_TILE, TSIDE, PATCH, TILES_DEV, TSIDE, PATCH)
    return jnp.transpose(shaped, (1, 4, 2, 5, 3, 6, 0)).reshape(TILES, TT, PV)

def all_pixels(tiled):
    shaped = tiled.reshape(N_TILE, TILES_DEV, TSIDE, TSIDE, PATCH, PATCH, LATC)
    return jnp.transpose(shaped, (6, 0, 2, 4, 1, 3, 5)).reshape(LATC, HL, WL)

def reference(latent, observed, noise, cloudy, timestep, pos_embed, embed_w, mod_w, wq, wk, wv, wo, q_gain, k_gain, out_w, conv_w):
    step_now = timestep[0].astype(jnp.float32)
    cos_now, sin_now = plan(step_now)
    cos_prev, sin_prev = plan(step_now - STRIDE)
    time_code = time_features(step_now, FREQ)
    modulation = jnp.dot(time_code, mod_w, preferred_element_type=jnp.float32)
    shift_vec = modulation[:, :D]
    scale_vec = modulation[:, D:2 * D]
    gate_vec = modulation[:, 2 * D:]
    tile_tokens = all_tiles(latent.astype(jnp.bfloat16))
    chosen_ids = jnp.nonzero(cloudy, size=OWNERS)[0].astype(jnp.int32)
    chosen = tile_tokens[chosen_ids]

    def one_tile(single):
        return denoise_tiles(single[None], embed_w, pos_embed, shift_vec, scale_vec, gate_vec, wq, wk, wv, wo, q_gain, k_gain, out_w)[0]
    eps_chosen = lax.map(one_tile, chosen)
    eps_tiles = jnp.zeros((TILES, TT, PV), jnp.bfloat16).at[chosen_ids].set(eps_chosen)
    eps_latent = all_pixels(eps_tiles.astype(jnp.float32))
    grid = cloudy.reshape(N_TILE, TILES_DEV)
    cloud_pixels = jnp.repeat(jnp.repeat(grid, TPX, axis=0), TPX, axis=1) == 1
    raw_estimate = jnp.where(cloud_pixels[None], (latent - sin_now * eps_latent) / cos_now, observed)
    padded = jnp.pad(raw_estimate, ((0, 0), (1, 1), (1, 1)))
    blended = jnp.zeros_like(raw_estimate)
    for row_shift in range(3):
        for col_shift in range(3):
            window = padded[:, row_shift:row_shift + HL, col_shift:col_shift + WL]
            blended = blended + jnp.einsum('oc,chw->ohw', conv_w[3 * row_shift + col_shift], window, precision=lax.Precision.HIGHEST)
    row_pos = jnp.arange(HL) % TPX
    col_pos = jnp.arange(WL) % TPX
    seam_mask = ((row_pos == 0) | (row_pos == TPX - 1))[:, None] | ((col_pos == 0) | (col_pos == TPX - 1))[None, :]
    estimate = jnp.where(seam_mask[None], blended, raw_estimate)
    next_latent = cos_prev * estimate + sin_prev * noise
    return (estimate, next_latent)
```

```python
import math

import jax
import jax.numpy as jnp
from jax import lax
from jax.sharding import Mesh
from jax.sharding import PartitionSpec as P

HD = 128
PATCH = 2
MAXOWN = 3
TSTEPS = 1000
STRIDE = 20
TILE = ("chip", "core")


def swap(x):
    return lax.ppermute(x, "core", [(0, 1), (1, 0)])


def in_order(c, mine, other, axis):
    lo = jnp.where(c == 0, mine, other)
    hi = jnp.where(c == 0, other, mine)
    return jnp.concatenate([lo, hi], axis=axis)


def padded_2(block, width):
    count = lax.axis_size("chip") * lax.axis_size("core")
    forward = [(i, i + 1) for i in range(count - 1)]
    backward = [(target, source) for source, target in forward]
    dim = 1
    low = lax.ppermute(
        lax.slice_in_dim(block, block.shape[dim] - width, None, axis=dim), TILE, forward
    )
    high = lax.ppermute(lax.slice_in_dim(block, 0, width, axis=dim), TILE, backward)
    return jnp.concatenate([low, block, high], axis=dim)


def plan(step):
    theta = (step / TSTEPS + 0.008) / 1.008 * (math.pi / 2)
    return (jnp.cos(theta), jnp.sin(theta))


def time_features(step, width):
    half = width // 2
    freqs = jnp.exp(-math.log(10000.0) * jnp.arange(half, dtype=jnp.float32) / half)
    angles = step * freqs
    code = jnp.concatenate([jnp.cos(angles), jnp.sin(angles)])[None, :]
    return jax.nn.silu(code).astype(jnp.bfloat16)


def layer_norm(values):
    center = values - jnp.mean(values, axis=-1, keepdims=True)
    spread = jnp.mean(center * center, axis=-1, keepdims=True)
    return center * lax.rsqrt(spread + 1e-06)


def head_norm(proj, gain, count, tokens_tile):
    shaped = proj.reshape(count, tokens_tile, -1, HD)
    scaled = shaped * lax.rsqrt(jnp.mean(shaped * shaped, axis=-1, keepdims=True) + 1e-06)
    return (scaled * gain).astype(jnp.bfloat16)


def band_tiles(band, tile_side):
    channels, band_rows, band_cols = band.shape
    tiles_here = band_cols // (tile_side * PATCH)
    shaped = band.reshape(channels, tile_side, PATCH, tiles_here, tile_side, PATCH)
    return jnp.transpose(shaped, (3, 1, 4, 2, 5, 0)).reshape(
        tiles_here, tile_side * tile_side, PATCH * PATCH * channels
    )


def band_pixels(tiled, tile_side, channels):
    tiles_here = tiled.shape[0]
    shaped = tiled.reshape(tiles_here, tile_side, tile_side, PATCH, PATCH, channels)
    return jnp.transpose(shaped, (5, 1, 3, 0, 2, 4)).reshape(
        channels, tile_side * PATCH, tiles_here * tile_side * PATCH
    )


def half_columns(w_local, c):
    half = w_local.shape[1] // 2
    mine = lax.dynamic_slice_in_dim(w_local, c * half, half, axis=1)
    other = lax.dynamic_slice_in_dim(w_local, (1 - c) * half, half, axis=1)
    return in_order(c, mine, swap(other), 0)


def my_features(x, c, n_chip):
    lead = x.shape[:-1]
    shaped = x.reshape(lead + (n_chip, 2, x.shape[-1] // (2 * n_chip)))
    picked = lax.dynamic_index_in_dim(shaped, c, axis=len(lead) + 1, keepdims=False)
    return picked.reshape(lead + (-1,))


def on_device(
    latent,
    observed,
    noise,
    cloudy,
    timestep,
    pos_embed,
    embed_w,
    mod_w,
    wq,
    wk,
    wv,
    wo,
    q_gain,
    k_gain,
    out_w,
    conv_w,
):
    c = lax.axis_index("core")
    n_chip = lax.axis_size("chip")
    channels, band_rows, band_cols = latent.shape
    tile_side = band_rows // PATCH
    tiles_here = band_cols // band_rows
    width = embed_w.shape[1]

    wq_h = lax.all_gather(half_columns(wq, c), "chip", axis=0, tiled=True)
    wk_h = lax.all_gather(half_columns(wk, c), "chip", axis=0, tiled=True)
    wv_h = lax.all_gather(half_columns(wv, c), "chip", axis=0, tiled=True)
    wo_c = lax.all_gather(wo, "chip", axis=1, tiled=True)

    step_now = timestep[0].astype(jnp.float32)
    cos_now, sin_now = plan(step_now)
    cos_prev, sin_prev = plan(step_now - STRIDE)
    time_code = time_features(step_now, mod_w.shape[0])
    local_mod = jnp.dot(time_code, mod_w, preferred_element_type=jnp.float32)
    modulation = lax.all_gather(local_mod, TILE, axis=1, tiled=True)
    shift_vec = modulation[:, :width]
    scale_vec = modulation[:, width : 2 * width]
    gate_vec = modulation[:, 2 * width :]

    tile_tokens = band_tiles(latent.astype(jnp.bfloat16), tile_side)
    order_in = jnp.cumsum(cloudy) - cloudy
    slot_ids = jnp.arange(MAXOWN, dtype=jnp.int32)
    slot_hit = (cloudy[None, :] == 1) & (order_in[None, :] == slot_ids[:, None])
    picked = jnp.sum(
        jnp.where(slot_hit, jnp.arange(tiles_here, dtype=jnp.int32)[None, :], 0), axis=1
    )
    chosen = jnp.take(tile_tokens, picked, axis=0)
    pair = in_order(c, chosen, swap(chosen), 0)

    count, tokens_tile, token_values = pair.shape
    row_count = count * tokens_tile
    flat = pair.reshape(row_count, token_values)
    hidden0 = jnp.dot(flat, embed_w, preferred_element_type=jnp.float32).reshape(
        count, tokens_tile, -1
    )
    hidden0 = (hidden0 + pos_embed.astype(jnp.float32)[None]).reshape(row_count, -1)
    modulated = (layer_norm(hidden0) * (1.0 + scale_vec) + shift_vec).astype(jnp.bfloat16)

    query_all = jnp.dot(modulated, wq_h, preferred_element_type=jnp.float32)
    key_all = jnp.dot(modulated, wk_h, preferred_element_type=jnp.float32)
    value_all = jnp.dot(modulated, wv_h, preferred_element_type=jnp.float32)
    query_norm = head_norm(query_all, q_gain, count, tokens_tile)
    key_norm = head_norm(key_all, k_gain, count, tokens_tile)
    value_half = value_all.reshape(count, tokens_tile, -1, HD).astype(jnp.bfloat16)
    scores = jnp.einsum(
        "nqhd,nkhd->nhqk", query_norm, key_norm, preferred_element_type=jnp.float32
    ) * HD ** (-0.5)
    peak = jnp.max(scores, axis=-1, keepdims=True)
    expo = jnp.exp(scores - peak)
    probs = (expo / jnp.sum(expo, axis=-1, keepdims=True)).astype(jnp.bfloat16)
    mixed = jnp.einsum("nhqk,nkhd->nqhd", probs, value_half, preferred_element_type=jnp.float32)
    mixed = mixed.astype(jnp.bfloat16).reshape(row_count, -1)
    mixed_all = in_order(c, mixed, swap(mixed), 1)

    attn_c = jnp.dot(mixed_all, wo_c, preferred_element_type=jnp.float32)
    hidden1 = my_features(hidden0, c, n_chip) + my_features(gate_vec, c, n_chip) * attn_c
    total = jnp.sum(hidden1, axis=-1, keepdims=True)
    center = hidden1 - (total + swap(total)) / width
    spread = jnp.sum(center * center, axis=-1, keepdims=True)
    final = (center * lax.rsqrt((spread + swap(spread)) / width + 1e-06)).astype(jnp.bfloat16)
    out_c = my_features(out_w.T, c, n_chip).T
    eps_part = jnp.dot(final, out_c, preferred_element_type=jnp.float32).reshape(
        count, tokens_tile, -1
    )
    own = lax.dynamic_slice_in_dim(eps_part, c * MAXOWN, MAXOWN, axis=0)
    theirs = lax.dynamic_slice_in_dim(eps_part, (1 - c) * MAXOWN, MAXOWN, axis=0)
    eps_chosen = (own + swap(theirs)).astype(jnp.bfloat16)

    eps_back = jnp.take(eps_chosen, jnp.minimum(order_in, MAXOWN - 1), axis=0)
    eps_tiles = jnp.where(cloudy[:, None, None] == 1, eps_back, jnp.zeros_like(eps_back))
    eps_latent = band_pixels(eps_tiles.astype(jnp.float32), tile_side, channels)
    cloud_cols = jnp.repeat(cloudy, band_rows) == 1
    raw_estimate = jnp.where(
        cloud_cols[None, None, :], (latent - sin_now * eps_latent) / cos_now, observed
    )
    padded = padded_2(raw_estimate, 1)
    padded = jnp.pad(padded, ((0, 0), (0, 0), (1, 1)))
    blended = jnp.zeros_like(raw_estimate)
    for row_shift in range(3):
        for col_shift in range(3):
            window = padded[:, row_shift : row_shift + band_rows, col_shift : col_shift + band_cols]
            blended = blended + jnp.einsum(
                "oc,chw->ohw",
                conv_w[3 * row_shift + col_shift],
                window,
                precision=lax.Precision.HIGHEST,
            )
    row_pos = jnp.arange(band_rows) % band_rows
    col_pos = jnp.arange(band_cols) % band_rows
    seam_mask = ((row_pos == 0) | (row_pos == band_rows - 1))[:, None] | (
        (col_pos == 0) | (col_pos == band_rows - 1)
    )[None, :]
    estimate = jnp.where(seam_mask[None], blended, raw_estimate)
    next_latent = cos_prev * estimate + sin_prev * noise
    return (estimate, next_latent)


def solution(mesh):
    devices = mesh.devices
    groups, tiles = devices.shape
    split = Mesh(devices.reshape(groups, tiles // 2, 2), ("grp",) + TILE)
    band = P(None, ("grp",) + TILE, None)
    placed = (
        band,
        band,
        band,
        P(("grp",) + TILE),
        P("grp"),
        P(),
        P(),
        P(None, TILE),
        P(TILE, None),
        P(TILE, None),
        P(TILE, None),
        P(None, TILE),
        P(),
        P(),
        P(),
        P(),
    )
    return jax.shard_map(
        on_device,
        mesh=split,
        in_specs=placed,
        out_specs=(band, band),
        check_vma=False,
    )
```

```python
import math

import jax
import jax.numpy as jnp
from jax import lax
from jax.sharding import Mesh
from jax.sharding import PartitionSpec as P

HD = 128
PATCH = 2
MAXOWN = 3
TSTEPS = 1000
STRIDE = 20
TILE = ("chip", "core")


def swap(x):
    return lax.ppermute(x, "core", [(0, 1), (1, 0)])


def in_order(c, mine, other, axis):
    lo = jnp.where(c == 0, mine, other)
    hi = jnp.where(c == 0, other, mine)
    return jnp.concatenate([lo, hi], axis=axis)


def padded_2(block, width):
    count = lax.axis_size("chip") * lax.axis_size("core")
    forward = [(i, i + 1) for i in range(count - 1)]
    backward = [(target, source) for source, target in forward]
    dim = 1
    low = lax.ppermute(
        lax.slice_in_dim(block, block.shape[dim] - width, None, axis=dim), TILE, forward
    )
    high = lax.ppermute(lax.slice_in_dim(block, 0, width, axis=dim), TILE, backward)
    return jnp.concatenate([low, block, high], axis=dim)


def plan(step):
    theta = (step / TSTEPS + 0.008) / 1.008 * (math.pi / 2)
    return (jnp.cos(theta), jnp.sin(theta))


def time_features(step, width):
    half = width // 2
    freqs = jnp.exp(-math.log(10000.0) * jnp.arange(half, dtype=jnp.float32) / half)
    angles = step * freqs
    code = jnp.concatenate([jnp.cos(angles), jnp.sin(angles)])[None, :]
    return jax.nn.silu(code).astype(jnp.bfloat16)


def layer_norm(values):
    center = values - jnp.mean(values, axis=-1, keepdims=True)
    spread = jnp.mean(center * center, axis=-1, keepdims=True)
    return center * lax.rsqrt(spread + 1e-06)


def head_norm(proj, gain, count, tokens_tile):
    shaped = proj.reshape(count, tokens_tile, -1, HD)
    scaled = shaped * lax.rsqrt(jnp.mean(shaped * shaped, axis=-1, keepdims=True) + 1e-06)
    return (scaled * gain).astype(jnp.bfloat16)


def band_tiles(band, tile_side):
    channels, band_rows, band_cols = band.shape
    tiles_here = band_cols // (tile_side * PATCH)
    shaped = band.reshape(channels, tile_side, PATCH, tiles_here, tile_side, PATCH)
    return jnp.transpose(shaped, (3, 1, 4, 2, 5, 0)).reshape(
        tiles_here, tile_side * tile_side, PATCH * PATCH * channels
    )


def band_pixels(tiled, tile_side, channels):
    tiles_here = tiled.shape[0]
    shaped = tiled.reshape(tiles_here, tile_side, tile_side, PATCH, PATCH, channels)
    return jnp.transpose(shaped, (5, 1, 3, 0, 2, 4)).reshape(
        channels, tile_side * PATCH, tiles_here * tile_side * PATCH
    )


def half_columns(w_local, c):
    half = w_local.shape[1] // 2
    mine = lax.dynamic_slice_in_dim(w_local, c * half, half, axis=1)
    other = lax.dynamic_slice_in_dim(w_local, (1 - c) * half, half, axis=1)
    return in_order(c, mine, swap(other), 0)


def my_features(x, c, n_chip):
    lead = x.shape[:-1]
    shaped = x.reshape(lead + (n_chip, 2, x.shape[-1] // (2 * n_chip)))
    picked = lax.dynamic_index_in_dim(shaped, c, axis=len(lead) + 1, keepdims=False)
    return picked.reshape(lead + (-1,))


def exact_parts(values):
    hi = lax.reduce_precision(values, exponent_bits=8, mantissa_bits=7)
    rest = values - hi
    mid = lax.reduce_precision(rest, exponent_bits=8, mantissa_bits=7)
    parts = (hi, mid, rest - mid)
    return jnp.stack([p.astype(jnp.bfloat16) for p in parts])


def on_device(
    latent,
    observed,
    noise,
    cloudy,
    timestep,
    pos_embed,
    embed_w,
    mod_w,
    wq,
    wk,
    wv,
    wo,
    q_gain,
    k_gain,
    out_w,
    conv_w,
):
    c = lax.axis_index("core")
    n_chip = lax.axis_size("chip")
    channels, band_rows, band_cols = latent.shape
    tile_side = band_rows // PATCH
    tiles_here = band_cols // band_rows
    width = embed_w.shape[1]

    step_now = timestep[0].astype(jnp.float32)
    cos_now, sin_now = plan(step_now)
    cos_prev, sin_prev = plan(step_now - STRIDE)
    time_code = time_features(step_now, mod_w.shape[0])
    local_mod = jnp.dot(time_code, mod_w, preferred_element_type=jnp.float32)
    mod_parts = exact_parts(in_order(c, local_mod, swap(local_mod), 0))

    half = wq.shape[1] // 2
    pieces = [half_columns(w, c) for w in (wq, wk, wv)]
    wo_rows = wo.reshape(-1, half)
    mod_flat = mod_parts.reshape(-1)
    mod_rows = jnp.pad(mod_flat, (0, (-mod_flat.shape[0]) % (8 * half))).reshape(-1, half)
    got = lax.all_gather(jnp.concatenate(pieces + [wo_rows, mod_rows], axis=0), "chip", axis=0)
    r2 = pieces[0].shape[0]
    wq_h, wk_h, wv_h = (got[:, i * r2 : (i + 1) * r2].reshape(-1, half) for i in range(3))
    wo_end = 3 * r2 + wo_rows.shape[0]
    wo_g = got[:, 3 * r2 : wo_end].reshape((n_chip,) + wo.shape)
    wo_c = jnp.transpose(wo_g, (1, 0, 2)).reshape(wo.shape[0], -1)
    mod_g = got[:, wo_end:].reshape(n_chip, -1)[:, : mod_flat.shape[0]]
    mod_g = mod_g.reshape((n_chip,) + mod_parts.shape).astype(jnp.float32)
    modulation = ((mod_g[:, 0] + mod_g[:, 1]) + mod_g[:, 2]).reshape(1, -1)
    shift_vec = modulation[:, :width]
    scale_vec = modulation[:, width : 2 * width]
    gate_vec = modulation[:, 2 * width :]

    tile_tokens = band_tiles(latent.astype(jnp.bfloat16), tile_side)
    order_in = jnp.cumsum(cloudy) - cloudy
    slot_ids = jnp.arange(MAXOWN, dtype=jnp.int32)
    slot_hit = (cloudy[None, :] == 1) & (order_in[None, :] == slot_ids[:, None])
    picked = jnp.sum(
        jnp.where(slot_hit, jnp.arange(tiles_here, dtype=jnp.int32)[None, :], 0), axis=1
    )
    chosen = jnp.take(tile_tokens, picked, axis=0)
    pair = in_order(c, chosen, swap(chosen), 0)

    count, tokens_tile, token_values = pair.shape
    row_count = count * tokens_tile
    flat = pair.reshape(row_count, token_values)
    hidden0 = jnp.dot(flat, embed_w, preferred_element_type=jnp.float32).reshape(
        count, tokens_tile, -1
    )
    hidden0 = (hidden0 + pos_embed.astype(jnp.float32)[None]).reshape(row_count, -1)
    modulated = (layer_norm(hidden0) * (1.0 + scale_vec) + shift_vec).astype(jnp.bfloat16)

    query_all = jnp.dot(modulated, wq_h, preferred_element_type=jnp.float32)
    key_all = jnp.dot(modulated, wk_h, preferred_element_type=jnp.float32)
    value_all = jnp.dot(modulated, wv_h, preferred_element_type=jnp.float32)
    query_norm = head_norm(query_all, q_gain, count, tokens_tile)
    key_norm = head_norm(key_all, k_gain, count, tokens_tile)
    value_half = value_all.reshape(count, tokens_tile, -1, HD).astype(jnp.bfloat16)
    scores = jnp.einsum(
        "nqhd,nkhd->nhqk", query_norm, key_norm, preferred_element_type=jnp.float32
    ) * HD ** (-0.5)
    peak = jnp.max(scores, axis=-1, keepdims=True)
    expo = jnp.exp(scores - peak)
    probs = (expo / jnp.sum(expo, axis=-1, keepdims=True)).astype(jnp.bfloat16)
    mixed = jnp.einsum("nhqk,nkhd->nqhd", probs, value_half, preferred_element_type=jnp.float32)
    mixed = mixed.astype(jnp.bfloat16).reshape(row_count, -1)
    mixed_all = in_order(c, mixed, swap(mixed), 1)

    attn_c = jnp.dot(mixed_all, wo_c, preferred_element_type=jnp.float32)
    hidden0_c = jnp.dot(flat, my_features(embed_w, c, n_chip), preferred_element_type=jnp.float32)
    pos_c = my_features(pos_embed, c, n_chip).astype(jnp.float32)
    hidden0_c = (hidden0_c.reshape(count, tokens_tile, -1) + pos_c[None]).reshape(row_count, -1)
    hidden1 = hidden0_c + my_features(gate_vec, c, n_chip) * attn_c
    total = jnp.sum(hidden1, axis=-1, keepdims=True)
    center = hidden1 - (total + swap(total)) / width
    spread = jnp.sum(center * center, axis=-1, keepdims=True)
    final = (center * lax.rsqrt((spread + swap(spread)) / width + 1e-06)).astype(jnp.bfloat16)
    out_c = my_features(out_w.T, c, n_chip).T
    eps_part = jnp.dot(final, out_c, preferred_element_type=jnp.float32).reshape(
        count, tokens_tile, -1
    )
    own = lax.dynamic_slice_in_dim(eps_part, c * MAXOWN, MAXOWN, axis=0)
    theirs = lax.dynamic_slice_in_dim(eps_part, (1 - c) * MAXOWN, MAXOWN, axis=0)
    eps_chosen = (own + swap(theirs)).astype(jnp.bfloat16)

    eps_back = jnp.take(eps_chosen, jnp.minimum(order_in, MAXOWN - 1), axis=0)
    eps_tiles = jnp.where(cloudy[:, None, None] == 1, eps_back, jnp.zeros_like(eps_back))
    eps_latent = band_pixels(eps_tiles.astype(jnp.float32), tile_side, channels)
    cloud_cols = jnp.repeat(cloudy, band_rows) == 1
    raw_estimate = jnp.where(
        cloud_cols[None, None, :], (latent - sin_now * eps_latent) / cos_now, observed
    )
    padded = padded_2(raw_estimate, 1)
    padded = jnp.pad(padded, ((0, 0), (0, 0), (1, 1)))
    blended = jnp.zeros_like(raw_estimate)
    for row_shift in range(3):
        for col_shift in range(3):
            window = padded[:, row_shift : row_shift + band_rows, col_shift : col_shift + band_cols]
            blended = blended + jnp.einsum(
                "oc,chw->ohw",
                conv_w[3 * row_shift + col_shift],
                window,
                precision=lax.Precision.HIGHEST,
            )
    row_pos = jnp.arange(band_rows) % band_rows
    col_pos = jnp.arange(band_cols) % band_rows
    seam_mask = ((row_pos == 0) | (row_pos == band_rows - 1))[:, None] | (
        (col_pos == 0) | (col_pos == band_rows - 1)
    )[None, :]
    estimate = jnp.where(seam_mask[None], blended, raw_estimate)
    next_latent = cos_prev * estimate + sin_prev * noise
    return (estimate, next_latent)


def solution(mesh):
    devices = mesh.devices
    groups, tiles = devices.shape
    split = Mesh(devices.reshape(groups, tiles // 2, 2), ("grp",) + TILE)
    band = P(None, ("grp",) + TILE, None)
    placed = (
        band,
        band,
        band,
        P(("grp",) + TILE),
        P("grp"),
        P(),
        P(),
        P(None, TILE),
        P(TILE, None),
        P(TILE, None),
        P(TILE, None),
        P(None, TILE),
        P(),
        P(),
        P(),
        P(),
    )
    return jax.shard_map(
        on_device,
        mesh=split,
        in_specs=placed,
        out_specs=(band, band),
        check_vma=False,
    )
```

```python
import math

import jax
import jax.numpy as jnp
from jax import lax
from jax.sharding import PartitionSpec as P

HD = 128
PATCH = 2
MAXOWN = 3
TSTEPS = 1000
STRIDE = 20


def padded_2(block, sides, width):
    for axis, dim in sides:
        count = lax.axis_size(axis)
        forward = [(i, i + 1) for i in range(count - 1)]
        backward = [(target, source) for source, target in forward]
        low = lax.ppermute(
            lax.slice_in_dim(block, block.shape[dim] - width, None, axis=dim), axis, forward
        )
        high = lax.ppermute(lax.slice_in_dim(block, 0, width, axis=dim), axis, backward)
        block = jnp.concatenate([low, block, high], axis=dim)
    return block


def plan(step):
    theta = (step / TSTEPS + 0.008) / 1.008 * (math.pi / 2)
    return (jnp.cos(theta), jnp.sin(theta))


def time_features(step, width):
    half = width // 2
    freqs = jnp.exp(-math.log(10000.0) * jnp.arange(half, dtype=jnp.float32) / half)
    angles = step * freqs
    code = jnp.concatenate([jnp.cos(angles), jnp.sin(angles)])[None, :]
    return jax.nn.silu(code).astype(jnp.bfloat16)


def layer_norm(values):
    center = values - jnp.mean(values, axis=-1, keepdims=True)
    spread = jnp.mean(center * center, axis=-1, keepdims=True)
    return center * lax.rsqrt(spread + 1e-06)


def head_norm(proj, gain, count, tokens_tile):
    shaped = proj.reshape(count, tokens_tile, -1, HD)
    scaled = shaped * lax.rsqrt(jnp.mean(shaped * shaped, axis=-1, keepdims=True) + 1e-06)
    return (scaled * gain).astype(jnp.bfloat16)


def band_tiles(band, tile_side):
    channels, band_rows, band_cols = band.shape
    tiles_here = band_cols // (tile_side * PATCH)
    shaped = band.reshape(channels, tile_side, PATCH, tiles_here, tile_side, PATCH)
    return jnp.transpose(shaped, (3, 1, 4, 2, 5, 0)).reshape(
        tiles_here, tile_side * tile_side, PATCH * PATCH * channels
    )


def band_pixels(tiled, tile_side, channels):
    tiles_here = tiled.shape[0]
    shaped = tiled.reshape(tiles_here, tile_side, tile_side, PATCH, PATCH, channels)
    return jnp.transpose(shaped, (5, 1, 3, 0, 2, 4)).reshape(
        channels, tile_side * PATCH, tiles_here * tile_side * PATCH
    )


def add_rows(left, shard_rows):
    return jnp.dot(left, shard_rows, preferred_element_type=jnp.float32)


def denoise(
    chosen,
    embed_w,
    pos_embed,
    shift_vec,
    scale_vec,
    gate_vec,
    wq,
    wk,
    wv,
    wo,
    q_gain,
    k_gain,
    out_w,
):
    count, tokens_tile, token_values = chosen.shape
    row_count = count * tokens_tile
    flat = chosen.reshape(row_count, token_values)
    hidden0 = jnp.dot(flat, embed_w, preferred_element_type=jnp.float32).reshape(
        count, tokens_tile, -1
    )
    hidden0 = (hidden0 + pos_embed.astype(jnp.float32)[None]).reshape(row_count, -1)
    modulated = (layer_norm(hidden0) * (1.0 + scale_vec) + shift_vec).astype(jnp.bfloat16)

    def add_one(shard_rows):
        return add_rows(modulated, shard_rows)

    inner = wq.shape[1]
    qkv = lax.all_gather(jnp.concatenate([wq, wk, wv], axis=1), "tile", axis=0, tiled=True)
    qkv_all = add_one(qkv)
    query_all = qkv_all[:, :inner]
    key_all = qkv_all[:, inner : 2 * inner]
    value_all = qkv_all[:, 2 * inner :]
    query_norm = head_norm(query_all, q_gain, count, tokens_tile)
    key_norm = head_norm(key_all, k_gain, count, tokens_tile)
    value_half = value_all.reshape(count, tokens_tile, -1, HD).astype(jnp.bfloat16)
    scores = jnp.einsum(
        "nqhd,nkhd->nhqk", query_norm, key_norm, preferred_element_type=jnp.float32
    ) * HD ** (-0.5)
    peak = jnp.max(scores, axis=-1, keepdims=True)
    expo = jnp.exp(scores - peak)
    probs = (expo / jnp.sum(expo, axis=-1, keepdims=True)).astype(jnp.bfloat16)
    mixed = jnp.einsum("nhqk,nkhd->nqhd", probs, value_half, preferred_element_type=jnp.float32)
    mixed = mixed.astype(jnp.bfloat16).reshape(row_count, -1)
    attn_out = jnp.dot(
        mixed, lax.all_gather(wo, "tile", axis=1, tiled=True), preferred_element_type=jnp.float32
    )
    hidden1 = hidden0 + gate_vec * attn_out
    final = layer_norm(hidden1).astype(jnp.bfloat16)
    eps_pred = jnp.dot(final, out_w, preferred_element_type=jnp.float32).astype(jnp.bfloat16)
    return eps_pred.reshape(count, tokens_tile, token_values)


def on_device(
    latent,
    observed,
    noise,
    cloudy,
    timestep,
    pos_embed,
    embed_w,
    mod_w,
    wq,
    wk,
    wv,
    wo,
    q_gain,
    k_gain,
    out_w,
    conv_w,
):
    channels, band_rows, band_cols = latent.shape
    tile_side = band_rows // PATCH
    tiles_here = band_cols // band_rows
    width = embed_w.shape[1]
    step_now = timestep[0].astype(jnp.float32)
    cos_now, sin_now = plan(step_now)
    cos_prev, sin_prev = plan(step_now - STRIDE)
    time_code = time_features(step_now, mod_w.shape[0])
    local_mod = jnp.dot(time_code, mod_w, preferred_element_type=jnp.float32)
    modulation = lax.all_gather(local_mod, "tile", axis=1, tiled=True)
    shift_vec = modulation[:, :width]
    scale_vec = modulation[:, width : 2 * width]
    gate_vec = modulation[:, 2 * width :]
    tile_tokens = band_tiles(latent.astype(jnp.bfloat16), tile_side)
    order_in = jnp.cumsum(cloudy) - cloudy
    weights_all = (
        embed_w,
        pos_embed,
        shift_vec,
        scale_vec,
        gate_vec,
        wq,
        wk,
        wv,
        wo,
        q_gain,
        k_gain,
        out_w,
    )
    slot_ids = jnp.arange(MAXOWN, dtype=jnp.int32)
    slot_hit = (cloudy[None, :] == 1) & (order_in[None, :] == slot_ids[:, None])
    picked = jnp.sum(
        jnp.where(slot_hit, jnp.arange(tiles_here, dtype=jnp.int32)[None, :], 0), axis=1
    )
    chosen = jnp.take(tile_tokens, picked, axis=0)
    eps_chosen = denoise(chosen, *weights_all)
    eps_back = jnp.take(eps_chosen, jnp.minimum(order_in, MAXOWN - 1), axis=0)
    eps_tiles = jnp.where(cloudy[:, None, None] == 1, eps_back, jnp.zeros_like(eps_back))
    eps_latent = band_pixels(eps_tiles.astype(jnp.float32), tile_side, channels)
    cloud_cols = jnp.repeat(cloudy, band_rows) == 1
    raw_estimate = jnp.where(
        cloud_cols[None, None, :], (latent - sin_now * eps_latent) / cos_now, observed
    )
    padded = padded_2(raw_estimate, (("tile", 1),), 1)
    padded = jnp.pad(padded, ((0, 0), (0, 0), (1, 1)))
    blended = jnp.zeros_like(raw_estimate)
    for row_shift in range(3):
        for col_shift in range(3):
            window = padded[:, row_shift : row_shift + band_rows, col_shift : col_shift + band_cols]
            blended = blended + jnp.einsum(
                "oc,chw->ohw",
                conv_w[3 * row_shift + col_shift],
                window,
                precision=lax.Precision.HIGHEST,
            )
    row_pos = jnp.arange(band_rows) % band_rows
    col_pos = jnp.arange(band_cols) % band_rows
    seam_mask = ((row_pos == 0) | (row_pos == band_rows - 1))[:, None] | (
        (col_pos == 0) | (col_pos == band_rows - 1)
    )[None, :]
    estimate = jnp.where(seam_mask[None], blended, raw_estimate)
    next_latent = cos_prev * estimate + sin_prev * noise
    return (estimate, next_latent)


def solution(mesh):
    placed = (
        P(None, ("grp", "tile"), None),
        P(None, ("grp", "tile"), None),
        P(None, ("grp", "tile"), None),
        P(("grp", "tile")),
        P("grp"),
        P(),
        P(),
        P(None, "tile"),
        P("tile", None),
        P("tile", None),
        P("tile", None),
        P(None, "tile"),
        P(),
        P(),
        P(),
        P(),
    )
    return jax.shard_map(
        on_device,
        mesh=mesh,
        in_specs=placed,
        out_specs=(P(None, ("grp", "tile"), None), P(None, ("grp", "tile"), None)),
        check_vma=False,
    )
```

```python
import math

import jax
import jax.numpy as jnp
from jax import lax
from jax.sharding import PartitionSpec as P

HD = 128
PATCH = 2
MAXOWN = 3
TSTEPS = 1000
STRIDE = 20


def padded_2(block, sides, width):
    for axis, dim in sides:
        count = lax.axis_size(axis)
        forward = [(i, i + 1) for i in range(count - 1)]
        backward = [(target, source) for source, target in forward]
        low = lax.ppermute(
            lax.slice_in_dim(block, block.shape[dim] - width, None, axis=dim), axis, forward
        )
        high = lax.ppermute(lax.slice_in_dim(block, 0, width, axis=dim), axis, backward)
        block = jnp.concatenate([low, block, high], axis=dim)
    return block


def plan(step):
    theta = (step / TSTEPS + 0.008) / 1.008 * (math.pi / 2)
    return (jnp.cos(theta), jnp.sin(theta))


def time_features(step, width):
    half = width // 2
    freqs = jnp.exp(-math.log(10000.0) * jnp.arange(half, dtype=jnp.float32) / half)
    angles = step * freqs
    code = jnp.concatenate([jnp.cos(angles), jnp.sin(angles)])[None, :]
    return jax.nn.silu(code).astype(jnp.bfloat16)


def layer_norm(values):
    center = values - jnp.mean(values, axis=-1, keepdims=True)
    spread = jnp.mean(center * center, axis=-1, keepdims=True)
    return center * lax.rsqrt(spread + 1e-06)


def head_norm(proj, gain, count, tokens_tile):
    shaped = proj.reshape(count, tokens_tile, -1, HD)
    scaled = shaped * lax.rsqrt(jnp.mean(shaped * shaped, axis=-1, keepdims=True) + 1e-06)
    return (scaled * gain).astype(jnp.bfloat16)


def band_tiles(band, tile_side):
    channels, band_rows, band_cols = band.shape
    tiles_here = band_cols // (tile_side * PATCH)
    shaped = band.reshape(channels, tile_side, PATCH, tiles_here, tile_side, PATCH)
    return jnp.transpose(shaped, (3, 1, 4, 2, 5, 0)).reshape(
        tiles_here, tile_side * tile_side, PATCH * PATCH * channels
    )


def band_pixels(tiled, tile_side, channels):
    tiles_here = tiled.shape[0]
    shaped = tiled.reshape(tiles_here, tile_side, tile_side, PATCH, PATCH, channels)
    return jnp.transpose(shaped, (5, 1, 3, 0, 2, 4)).reshape(
        channels, tile_side * PATCH, tiles_here * tile_side * PATCH
    )


def spread_columns(w_local):
    count = lax.axis_size("tile")
    copies = jnp.broadcast_to(w_local[None], (count,) + w_local.shape)
    got = lax.all_to_all(copies, "tile", 0, 0, tiled=True)
    return jnp.transpose(got, (1, 0, 2)).reshape(w_local.shape[0], -1)


def add_rows(left, shard_rows):
    return jnp.dot(left, shard_rows, preferred_element_type=jnp.float32)


def denoise(
    chosen,
    embed_w,
    pos_embed,
    shift_vec,
    scale_vec,
    gate_vec,
    wq,
    wk,
    wv,
    wo,
    q_gain,
    k_gain,
    out_w,
):
    count, tokens_tile, token_values = chosen.shape
    row_count = count * tokens_tile
    flat = chosen.reshape(row_count, token_values)
    hidden0 = jnp.dot(flat, embed_w, preferred_element_type=jnp.float32).reshape(
        count, tokens_tile, -1
    )
    hidden0 = (hidden0 + pos_embed.astype(jnp.float32)[None]).reshape(row_count, -1)
    modulated = (layer_norm(hidden0) * (1.0 + scale_vec) + shift_vec).astype(jnp.bfloat16)

    def add_one(shard_rows):
        return add_rows(modulated, shard_rows)

    inner = wq.shape[1]
    qkv = lax.all_gather(jnp.concatenate([wq, wk, wv], axis=1), "tile", axis=0, tiled=True)
    qkv_all = add_one(qkv)
    query_all = qkv_all[:, :inner]
    key_all = qkv_all[:, inner : 2 * inner]
    value_all = qkv_all[:, 2 * inner :]
    query_norm = head_norm(query_all, q_gain, count, tokens_tile)
    key_norm = head_norm(key_all, k_gain, count, tokens_tile)
    value_half = value_all.reshape(count, tokens_tile, -1, HD).astype(jnp.bfloat16)
    scores = jnp.einsum(
        "nqhd,nkhd->nhqk", query_norm, key_norm, preferred_element_type=jnp.float32
    ) * HD ** (-0.5)
    peak = jnp.max(scores, axis=-1, keepdims=True)
    expo = jnp.exp(scores - peak)
    probs = (expo / jnp.sum(expo, axis=-1, keepdims=True)).astype(jnp.bfloat16)
    mixed = jnp.einsum("nhqk,nkhd->nqhd", probs, value_half, preferred_element_type=jnp.float32)
    mixed = mixed.astype(jnp.bfloat16).reshape(row_count, -1)
    attn_out = jnp.dot(mixed, spread_columns(wo), preferred_element_type=jnp.float32)
    hidden1 = hidden0 + gate_vec * attn_out
    final = layer_norm(hidden1).astype(jnp.bfloat16)
    eps_pred = jnp.dot(final, out_w, preferred_element_type=jnp.float32).astype(jnp.bfloat16)
    return eps_pred.reshape(count, tokens_tile, token_values)


def on_device(
    latent,
    observed,
    noise,
    cloudy,
    timestep,
    pos_embed,
    embed_w,
    mod_w,
    wq,
    wk,
    wv,
    wo,
    q_gain,
    k_gain,
    out_w,
    conv_w,
):
    channels, band_rows, band_cols = latent.shape
    tile_side = band_rows // PATCH
    tiles_here = band_cols // band_rows
    width = embed_w.shape[1]
    step_now = timestep[0].astype(jnp.float32)
    cos_now, sin_now = plan(step_now)
    cos_prev, sin_prev = plan(step_now - STRIDE)
    time_code = time_features(step_now, mod_w.shape[0])
    local_mod = jnp.dot(time_code, mod_w, preferred_element_type=jnp.float32)
    modulation = lax.all_gather(local_mod, "tile", axis=1, tiled=True)
    shift_vec = modulation[:, :width]
    scale_vec = modulation[:, width : 2 * width]
    gate_vec = modulation[:, 2 * width :]
    tile_tokens = band_tiles(latent.astype(jnp.bfloat16), tile_side)
    order_in = jnp.cumsum(cloudy) - cloudy
    weights_all = (
        embed_w,
        pos_embed,
        shift_vec,
        scale_vec,
        gate_vec,
        wq,
        wk,
        wv,
        wo,
        q_gain,
        k_gain,
        out_w,
    )
    slot_ids = jnp.arange(MAXOWN, dtype=jnp.int32)
    slot_hit = (cloudy[None, :] == 1) & (order_in[None, :] == slot_ids[:, None])
    picked = jnp.sum(
        jnp.where(slot_hit, jnp.arange(tiles_here, dtype=jnp.int32)[None, :], 0), axis=1
    )
    chosen = jnp.take(tile_tokens, picked, axis=0)
    eps_chosen = denoise(chosen, *weights_all)
    eps_back = jnp.take(eps_chosen, jnp.minimum(order_in, MAXOWN - 1), axis=0)
    eps_tiles = jnp.where(cloudy[:, None, None] == 1, eps_back, jnp.zeros_like(eps_back))
    eps_latent = band_pixels(eps_tiles.astype(jnp.float32), tile_side, channels)
    cloud_cols = jnp.repeat(cloudy, band_rows) == 1
    raw_estimate = jnp.where(
        cloud_cols[None, None, :], (latent - sin_now * eps_latent) / cos_now, observed
    )
    padded = padded_2(raw_estimate, (("tile", 1),), 1)
    padded = jnp.pad(padded, ((0, 0), (0, 0), (1, 1)))
    blended = jnp.zeros_like(raw_estimate)
    for row_shift in range(3):
        for col_shift in range(3):
            window = padded[:, row_shift : row_shift + band_rows, col_shift : col_shift + band_cols]
            blended = blended + jnp.einsum(
                "oc,chw->ohw",
                conv_w[3 * row_shift + col_shift],
                window,
                precision=lax.Precision.HIGHEST,
            )
    row_pos = jnp.arange(band_rows) % band_rows
    col_pos = jnp.arange(band_cols) % band_rows
    seam_mask = ((row_pos == 0) | (row_pos == band_rows - 1))[:, None] | (
        (col_pos == 0) | (col_pos == band_rows - 1)
    )[None, :]
    estimate = jnp.where(seam_mask[None], blended, raw_estimate)
    next_latent = cos_prev * estimate + sin_prev * noise
    return (estimate, next_latent)


def solution(mesh):
    placed = (
        P(None, ("grp", "tile"), None),
        P(None, ("grp", "tile"), None),
        P(None, ("grp", "tile"), None),
        P(("grp", "tile")),
        P("grp"),
        P(),
        P(),
        P(None, "tile"),
        P("tile", None),
        P("tile", None),
        P("tile", None),
        P(None, "tile"),
        P(),
        P(),
        P(),
        P(),
    )
    return jax.shard_map(
        on_device,
        mesh=mesh,
        in_specs=placed,
        out_specs=(P(None, ("grp", "tile"), None), P(None, ("grp", "tile"), None)),
        check_vma=False,
    )
```

```python
import math

import jax
import jax.numpy as jnp
from jax import lax
from jax.sharding import PartitionSpec as P

HD = 128
PATCH = 2
MAXOWN = 3
TSTEPS = 1000
STRIDE = 20


def plan(step):
    theta = (step / TSTEPS + 0.008) / 1.008 * (math.pi / 2)
    return (jnp.cos(theta), jnp.sin(theta))


def time_features(step, width):
    half = width // 2
    freqs = jnp.exp(-math.log(10000.0) * jnp.arange(half, dtype=jnp.float32) / half)
    angles = step * freqs
    code = jnp.concatenate([jnp.cos(angles), jnp.sin(angles)])[None, :]
    return jax.nn.silu(code).astype(jnp.bfloat16)


def layer_norm(values):
    center = values - jnp.mean(values, axis=-1, keepdims=True)
    spread = jnp.mean(center * center, axis=-1, keepdims=True)
    return center * lax.rsqrt(spread + 1e-06)


def head_norm(proj, gain, count, tokens_tile):
    shaped = proj.reshape(count, tokens_tile, -1, HD)
    scaled = shaped * lax.rsqrt(jnp.mean(shaped * shaped, axis=-1, keepdims=True) + 1e-06)
    return (scaled * gain).astype(jnp.bfloat16)


def band_tiles(band, tile_side):
    channels, band_rows, band_cols = band.shape
    tiles_here = band_cols // (tile_side * PATCH)
    shaped = band.reshape(channels, tile_side, PATCH, tiles_here, tile_side, PATCH)
    return jnp.transpose(shaped, (3, 1, 4, 2, 5, 0)).reshape(
        tiles_here, tile_side * tile_side, PATCH * PATCH * channels
    )


def band_pixels(tiled, tile_side, channels):
    tiles_here = tiled.shape[0]
    shaped = tiled.reshape(tiles_here, tile_side, tile_side, PATCH, PATCH, channels)
    return jnp.transpose(shaped, (5, 1, 3, 0, 2, 4)).reshape(
        channels, tile_side * PATCH, tiles_here * tile_side * PATCH
    )


def add_rows(left, shard_rows):
    return jnp.dot(left, shard_rows, preferred_element_type=jnp.float32)


def denoise(
    chosen,
    embed_w,
    pos_embed,
    shift_vec,
    scale_vec,
    gate_vec,
    wq,
    wk,
    wv,
    wo,
    q_gain,
    k_gain,
    out_w,
):
    count, tokens_tile, token_values = chosen.shape
    row_count = count * tokens_tile
    flat = chosen.reshape(row_count, token_values)
    hidden0 = jnp.dot(flat, embed_w, preferred_element_type=jnp.float32).reshape(
        count, tokens_tile, -1
    )
    hidden0 = (hidden0 + pos_embed.astype(jnp.float32)[None]).reshape(row_count, -1)
    modulated = (layer_norm(hidden0) * (1.0 + scale_vec) + shift_vec).astype(jnp.bfloat16)

    def add_one(shard_rows):
        return add_rows(modulated, shard_rows)

    inner = wq.shape[1]
    qkv = lax.all_gather(jnp.concatenate([wq, wk, wv], axis=1), "tile", axis=0, tiled=True)
    qkv_all = add_one(qkv)
    query_all = qkv_all[:, :inner]
    key_all = qkv_all[:, inner : 2 * inner]
    value_all = qkv_all[:, 2 * inner :]
    query_norm = head_norm(query_all, q_gain, count, tokens_tile)
    key_norm = head_norm(key_all, k_gain, count, tokens_tile)
    value_half = value_all.reshape(count, tokens_tile, -1, HD).astype(jnp.bfloat16)
    scores = jnp.einsum(
        "nqhd,nkhd->nhqk", query_norm, key_norm, preferred_element_type=jnp.float32
    ) * HD ** (-0.5)
    peak = jnp.max(scores, axis=-1, keepdims=True)
    expo = jnp.exp(scores - peak)
    probs = (expo / jnp.sum(expo, axis=-1, keepdims=True)).astype(jnp.bfloat16)
    mixed = jnp.einsum("nhqk,nkhd->nqhd", probs, value_half, preferred_element_type=jnp.float32)
    mixed = mixed.astype(jnp.bfloat16).reshape(row_count, -1)
    attn_out = jnp.dot(
        mixed, lax.all_gather(wo, "tile", axis=1, tiled=True), preferred_element_type=jnp.float32
    )
    hidden1 = hidden0 + gate_vec * attn_out
    final = layer_norm(hidden1).astype(jnp.bfloat16)
    eps_pred = jnp.dot(final, out_w, preferred_element_type=jnp.float32).astype(jnp.bfloat16)
    return eps_pred.reshape(count, tokens_tile, token_values)


def taps(conv_w, window, a, b):
    return jnp.einsum(
        "oc,c...->o...", conv_w[3 * a + b], window, precision=lax.Precision.HIGHEST
    )


def seam_blend(raw, conv_w, tile_px):
    channels, rows, cols = raw.shape
    count = lax.axis_size("tile")
    forward = [(i, i + 1) for i in range(count - 1)]
    backward = [(target, source) for source, target in forward]
    low = lax.ppermute(raw[:, rows - 1 :], "tile", forward)
    high = lax.ppermute(raw[:, :1], "tile", backward)

    seam_cols = [j for j in range(cols) if j % tile_px in (0, tile_px - 1)]
    framed = jnp.pad(raw, ((0, 0), (1, 1), (1, 1)))
    shifted = [jnp.stack([framed[:, :, j + b] for j in seam_cols], axis=-1) for b in range(3)]
    by_col = None
    for a in range(3):
        for b in range(3):
            term = taps(conv_w, shifted[b][:, a : a + rows], a, b)
            by_col = term if by_col is None else by_col + term

    edge = jnp.concatenate([low, raw[:, :2], raw[:, rows - 2 :], high], axis=1)
    edge = jnp.pad(edge, ((0, 0), (0, 0), (1, 1)))
    by_row = None
    for a in range(3):
        for b in range(3):
            window = jnp.stack([edge[:, a, b : b + cols], edge[:, 3 + a, b : b + cols]], axis=1)
            term = taps(conv_w, window, a, b)
            by_row = term if by_row is None else by_row + term

    pieces = []
    done = 0
    for k, j in enumerate(seam_cols):
        if j > done:
            pieces.append(raw[:, :, done:j])
        pieces.append(by_col[:, :, k : k + 1])
        done = j + 1
    if done < cols:
        pieces.append(raw[:, :, done:])
    mixed_cols = jnp.concatenate(pieces, axis=2)
    return jnp.concatenate(
        [by_row[:, :1], mixed_cols[:, 1 : rows - 1], by_row[:, 1:]], axis=1
    )


def on_device(
    latent,
    observed,
    noise,
    cloudy,
    timestep,
    pos_embed,
    embed_w,
    mod_w,
    wq,
    wk,
    wv,
    wo,
    q_gain,
    k_gain,
    out_w,
    conv_w,
):
    channels, band_rows, band_cols = latent.shape
    tile_side = band_rows // PATCH
    tiles_here = band_cols // band_rows
    width = embed_w.shape[1]
    step_now = timestep[0].astype(jnp.float32)
    cos_now, sin_now = plan(step_now)
    cos_prev, sin_prev = plan(step_now - STRIDE)
    time_code = time_features(step_now, mod_w.shape[0])
    local_mod = jnp.dot(time_code, mod_w, preferred_element_type=jnp.float32)
    modulation = lax.all_gather(local_mod, "tile", axis=1, tiled=True)
    shift_vec = modulation[:, :width]
    scale_vec = modulation[:, width : 2 * width]
    gate_vec = modulation[:, 2 * width :]
    tile_tokens = band_tiles(latent.astype(jnp.bfloat16), tile_side)
    order_in = jnp.cumsum(cloudy) - cloudy
    weights_all = (
        embed_w,
        pos_embed,
        shift_vec,
        scale_vec,
        gate_vec,
        wq,
        wk,
        wv,
        wo,
        q_gain,
        k_gain,
        out_w,
    )
    slot_ids = jnp.arange(MAXOWN, dtype=jnp.int32)
    slot_hit = (cloudy[None, :] == 1) & (order_in[None, :] == slot_ids[:, None])
    picked = jnp.sum(
        jnp.where(slot_hit, jnp.arange(tiles_here, dtype=jnp.int32)[None, :], 0), axis=1
    )
    chosen = jnp.take(tile_tokens, picked, axis=0)
    eps_chosen = denoise(chosen, *weights_all)
    eps_back = jnp.take(eps_chosen, jnp.minimum(order_in, MAXOWN - 1), axis=0)
    eps_tiles = jnp.where(cloudy[:, None, None] == 1, eps_back, jnp.zeros_like(eps_back))
    eps_latent = band_pixels(eps_tiles.astype(jnp.float32), tile_side, channels)
    cloud_cols = jnp.repeat(cloudy, band_rows) == 1
    raw_estimate = jnp.where(
        cloud_cols[None, None, :], (latent - sin_now * eps_latent) / cos_now, observed
    )
    estimate = seam_blend(raw_estimate, conv_w, band_rows)
    next_latent = cos_prev * estimate + sin_prev * noise
    return (estimate, next_latent)


def solution(mesh):
    placed = (
        P(None, ("grp", "tile"), None),
        P(None, ("grp", "tile"), None),
        P(None, ("grp", "tile"), None),
        P(("grp", "tile")),
        P("grp"),
        P(),
        P(),
        P(None, "tile"),
        P("tile", None),
        P("tile", None),
        P("tile", None),
        P(None, "tile"),
        P(),
        P(),
        P(),
        P(),
    )
    return jax.shard_map(
        on_device,
        mesh=mesh,
        in_specs=placed,
        out_specs=(P(None, ("grp", "tile"), None), P(None, ("grp", "tile"), None)),
        check_vma=False,
    )
```

```python
import math

import jax
import jax.numpy as jnp
from jax import lax
from jax.sharding import PartitionSpec as P

HD = 128
PATCH = 2
MAXOWN = 3
TSTEPS = 1000
STRIDE = 20


def padded_2(block, sides, width):
    for axis, dim in sides:
        count = lax.axis_size(axis)
        forward = [(i, i + 1) for i in range(count - 1)]
        backward = [(target, source) for source, target in forward]
        low = lax.ppermute(
            lax.slice_in_dim(block, block.shape[dim] - width, None, axis=dim), axis, forward
        )
        high = lax.ppermute(lax.slice_in_dim(block, 0, width, axis=dim), axis, backward)
        block = jnp.concatenate([low, block, high], axis=dim)
    return block


def plan(step):
    theta = (step / TSTEPS + 0.008) / 1.008 * (math.pi / 2)
    return (jnp.cos(theta), jnp.sin(theta))


def time_features(step, width):
    half = width // 2
    freqs = jnp.exp(-math.log(10000.0) * jnp.arange(half, dtype=jnp.float32) / half)
    angles = step * freqs
    code = jnp.concatenate([jnp.cos(angles), jnp.sin(angles)])[None, :]
    return jax.nn.silu(code).astype(jnp.bfloat16)


def layer_norm(values):
    center = values - jnp.mean(values, axis=-1, keepdims=True)
    spread = jnp.mean(center * center, axis=-1, keepdims=True)
    return center * lax.rsqrt(spread + 1e-06)


def head_norm(proj, gain, count, tokens_tile):
    shaped = proj.reshape(count, tokens_tile, -1, HD)
    scaled = shaped * lax.rsqrt(jnp.mean(shaped * shaped, axis=-1, keepdims=True) + 1e-06)
    return (scaled * gain).astype(jnp.bfloat16)


def band_tiles(band, tile_side):
    channels, band_rows, band_cols = band.shape
    tiles_here = band_cols // (tile_side * PATCH)
    shaped = band.reshape(channels, tile_side, PATCH, tiles_here, tile_side, PATCH)
    return jnp.transpose(shaped, (3, 1, 4, 2, 5, 0)).reshape(
        tiles_here, tile_side * tile_side, PATCH * PATCH * channels
    )


def band_pixels(tiled, tile_side, channels):
    tiles_here = tiled.shape[0]
    shaped = tiled.reshape(tiles_here, tile_side, tile_side, PATCH, PATCH, channels)
    return jnp.transpose(shaped, (5, 1, 3, 0, 2, 4)).reshape(
        channels, tile_side * PATCH, tiles_here * tile_side * PATCH
    )


def share_of_part(w_local):
    parts = lax.axis_size("grp")
    rows = w_local.shape[0] // parts
    return lax.dynamic_slice_in_dim(w_local, lax.axis_index("grp") * rows, rows, axis=0)


def add_rows(left, shard_rows):
    return jnp.dot(left, shard_rows, preferred_element_type=jnp.float32)


def denoise(
    chosen,
    embed_w,
    pos_embed,
    shift_vec,
    scale_vec,
    gate_vec,
    wq,
    wk,
    wv,
    wo,
    q_gain,
    k_gain,
    out_w,
):
    count, tokens_tile, token_values = chosen.shape
    row_count = count * tokens_tile
    flat = chosen.reshape(row_count, token_values)
    hidden0 = jnp.dot(flat, embed_w, preferred_element_type=jnp.float32).reshape(
        count, tokens_tile, -1
    )
    hidden0 = (hidden0 + pos_embed.astype(jnp.float32)[None]).reshape(row_count, -1)
    modulated = (layer_norm(hidden0) * (1.0 + scale_vec) + shift_vec).astype(jnp.bfloat16)

    def add_one(shard_rows):
        return add_rows(modulated, shard_rows)

    inner = wq.shape[1]
    qkv = lax.all_gather(share_of_part(jnp.concatenate([wq, wk, wv], axis=1)), ("tile", "grp"), axis=0, tiled=True)
    qkv_all = add_one(qkv)
    query_all = qkv_all[:, :inner]
    key_all = qkv_all[:, inner : 2 * inner]
    value_all = qkv_all[:, 2 * inner :]
    query_norm = head_norm(query_all, q_gain, count, tokens_tile)
    key_norm = head_norm(key_all, k_gain, count, tokens_tile)
    value_half = value_all.reshape(count, tokens_tile, -1, HD).astype(jnp.bfloat16)
    scores = jnp.einsum(
        "nqhd,nkhd->nhqk", query_norm, key_norm, preferred_element_type=jnp.float32
    ) * HD ** (-0.5)
    peak = jnp.max(scores, axis=-1, keepdims=True)
    expo = jnp.exp(scores - peak)
    probs = (expo / jnp.sum(expo, axis=-1, keepdims=True)).astype(jnp.bfloat16)
    mixed = jnp.einsum("nhqk,nkhd->nqhd", probs, value_half, preferred_element_type=jnp.float32)
    mixed = mixed.astype(jnp.bfloat16).reshape(row_count, -1)
    attn_out = jnp.dot(
        mixed, lax.all_gather(wo, "tile", axis=1, tiled=True), preferred_element_type=jnp.float32
    )
    hidden1 = hidden0 + gate_vec * attn_out
    final = layer_norm(hidden1).astype(jnp.bfloat16)
    eps_pred = jnp.dot(final, out_w, preferred_element_type=jnp.float32).astype(jnp.bfloat16)
    return eps_pred.reshape(count, tokens_tile, token_values)


def on_device(
    latent,
    observed,
    noise,
    cloudy,
    timestep,
    pos_embed,
    embed_w,
    mod_w,
    wq,
    wk,
    wv,
    wo,
    q_gain,
    k_gain,
    out_w,
    conv_w,
):
    channels, band_rows, band_cols = latent.shape
    tile_side = band_rows // PATCH
    tiles_here = band_cols // band_rows
    width = embed_w.shape[1]
    step_now = timestep[0].astype(jnp.float32)
    cos_now, sin_now = plan(step_now)
    cos_prev, sin_prev = plan(step_now - STRIDE)
    time_code = time_features(step_now, mod_w.shape[0])
    local_mod = jnp.dot(time_code, mod_w, preferred_element_type=jnp.float32)
    modulation = lax.all_gather(local_mod, "tile", axis=1, tiled=True)
    shift_vec = modulation[:, :width]
    scale_vec = modulation[:, width : 2 * width]
    gate_vec = modulation[:, 2 * width :]
    tile_tokens = band_tiles(latent.astype(jnp.bfloat16), tile_side)
    order_in = jnp.cumsum(cloudy) - cloudy
    weights_all = (
        embed_w,
        pos_embed,
        shift_vec,
        scale_vec,
        gate_vec,
        wq,
        wk,
        wv,
        wo,
        q_gain,
        k_gain,
        out_w,
    )
    slot_ids = jnp.arange(MAXOWN, dtype=jnp.int32)
    slot_hit = (cloudy[None, :] == 1) & (order_in[None, :] == slot_ids[:, None])
    picked = jnp.sum(
        jnp.where(slot_hit, jnp.arange(tiles_here, dtype=jnp.int32)[None, :], 0), axis=1
    )
    chosen = jnp.take(tile_tokens, picked, axis=0)
    eps_chosen = denoise(chosen, *weights_all)
    eps_back = jnp.take(eps_chosen, jnp.minimum(order_in, MAXOWN - 1), axis=0)
    eps_tiles = jnp.where(cloudy[:, None, None] == 1, eps_back, jnp.zeros_like(eps_back))
    eps_latent = band_pixels(eps_tiles.astype(jnp.float32), tile_side, channels)
    cloud_cols = jnp.repeat(cloudy, band_rows) == 1
    raw_estimate = jnp.where(
        cloud_cols[None, None, :], (latent - sin_now * eps_latent) / cos_now, observed
    )
    padded = padded_2(raw_estimate, (("tile", 1),), 1)
    padded = jnp.pad(padded, ((0, 0), (0, 0), (1, 1)))
    blended = jnp.zeros_like(raw_estimate)
    for row_shift in range(3):
        for col_shift in range(3):
            window = padded[:, row_shift : row_shift + band_rows, col_shift : col_shift + band_cols]
            blended = blended + jnp.einsum(
                "oc,chw->ohw",
                conv_w[3 * row_shift + col_shift],
                window,
                precision=lax.Precision.HIGHEST,
            )
    row_pos = jnp.arange(band_rows) % band_rows
    col_pos = jnp.arange(band_cols) % band_rows
    seam_mask = ((row_pos == 0) | (row_pos == band_rows - 1))[:, None] | (
        (col_pos == 0) | (col_pos == band_rows - 1)
    )[None, :]
    estimate = jnp.where(seam_mask[None], blended, raw_estimate)
    next_latent = cos_prev * estimate + sin_prev * noise
    return (estimate, next_latent)


def solution(mesh):
    placed = (
        P(None, ("grp", "tile"), None),
        P(None, ("grp", "tile"), None),
        P(None, ("grp", "tile"), None),
        P(("grp", "tile")),
        P("grp"),
        P(),
        P(),
        P(None, "tile"),
        P("tile", None),
        P("tile", None),
        P("tile", None),
        P(None, "tile"),
        P(),
        P(),
        P(),
        P(),
    )
    return jax.shard_map(
        on_device,
        mesh=mesh,
        in_specs=placed,
        out_specs=(P(None, ("grp", "tile"), None), P(None, ("grp", "tile"), None)),
        check_vma=False,
    )
```

```python
import math

import jax
import jax.numpy as jnp
from jax import lax
from jax.experimental import pallas as pl
from jax.experimental.pallas import tpu as pltpu
from jax.sharding import PartitionSpec as P

HD = 128
PATCH = 2
MAXOWN = 3
TSTEPS = 1000
STRIDE = 20


def plan(step):
    theta = (step / TSTEPS + 0.008) / 1.008 * (math.pi / 2)
    return (jnp.cos(theta), jnp.sin(theta))


def time_features(step, width):
    half = width // 2
    freqs = jnp.exp(-math.log(10000.0) * jnp.arange(half, dtype=jnp.float32) / half)
    angles = step * freqs
    code = jnp.concatenate([jnp.cos(angles), jnp.sin(angles)])[None, :]
    return jax.nn.silu(code).astype(jnp.bfloat16)


def layer_norm(values):
    center = values - jnp.mean(values, axis=-1, keepdims=True)
    spread = jnp.mean(center * center, axis=-1, keepdims=True)
    return center * lax.rsqrt(spread + 1e-06)


def head_norm(proj, gain, count, tokens_tile):
    shaped = proj.reshape(count, tokens_tile, -1, HD)
    scaled = shaped * lax.rsqrt(jnp.mean(shaped * shaped, axis=-1, keepdims=True) + 1e-06)
    return (scaled * gain).astype(jnp.bfloat16)


def band_tiles(band, tile_side):
    channels, band_rows, band_cols = band.shape
    tiles_here = band_cols // (tile_side * PATCH)
    shaped = band.reshape(channels, tile_side, PATCH, tiles_here, tile_side, PATCH)
    return jnp.transpose(shaped, (3, 1, 4, 2, 5, 0)).reshape(
        tiles_here, tile_side * tile_side, PATCH * PATCH * channels
    )


def band_pixels(tiled, tile_side, channels):
    tiles_here = tiled.shape[0]
    shaped = tiled.reshape(tiles_here, tile_side, tile_side, PATCH, PATCH, channels)
    return jnp.transpose(shaped, (5, 1, 3, 0, 2, 4)).reshape(
        channels, tile_side * PATCH, tiles_here * tile_side * PATCH
    )


def share_of_part(w_local):
    parts = lax.axis_size("grp")
    rows = w_local.shape[0] // parts
    return lax.dynamic_slice_in_dim(w_local, lax.axis_index("grp") * rows, rows, axis=0)


def add_rows(left, shard_rows):
    return jnp.dot(left, shard_rows, preferred_element_type=jnp.float32)


def denoise(
    chosen,
    embed_w,
    pos_embed,
    shift_vec,
    scale_vec,
    gate_vec,
    wq,
    wk,
    wv,
    wo,
    q_gain,
    k_gain,
    out_w,
):
    count, tokens_tile, token_values = chosen.shape
    row_count = count * tokens_tile
    flat = chosen.reshape(row_count, token_values)
    hidden0 = jnp.dot(flat, embed_w, preferred_element_type=jnp.float32).reshape(
        count, tokens_tile, -1
    )
    hidden0 = (hidden0 + pos_embed.astype(jnp.float32)[None]).reshape(row_count, -1)
    modulated = (layer_norm(hidden0) * (1.0 + scale_vec) + shift_vec).astype(jnp.bfloat16)

    def add_one(shard_rows):
        return add_rows(modulated, shard_rows)

    inner = wq.shape[1]
    qkv = lax.all_gather(share_of_part(jnp.concatenate([wq, wk, wv], axis=1)), ("tile", "grp"), axis=0, tiled=True)
    qkv_all = add_one(qkv)
    query_all = qkv_all[:, :inner]
    key_all = qkv_all[:, inner : 2 * inner]
    value_all = qkv_all[:, 2 * inner :]
    query_norm = head_norm(query_all, q_gain, count, tokens_tile)
    key_norm = head_norm(key_all, k_gain, count, tokens_tile)
    value_half = value_all.reshape(count, tokens_tile, -1, HD).astype(jnp.bfloat16)
    scores = jnp.einsum(
        "nqhd,nkhd->nhqk", query_norm, key_norm, preferred_element_type=jnp.float32
    ) * HD ** (-0.5)
    peak = jnp.max(scores, axis=-1, keepdims=True)
    expo = jnp.exp(scores - peak)
    probs = (expo / jnp.sum(expo, axis=-1, keepdims=True)).astype(jnp.bfloat16)
    mixed = jnp.einsum("nhqk,nkhd->nqhd", probs, value_half, preferred_element_type=jnp.float32)
    mixed = mixed.astype(jnp.bfloat16).reshape(row_count, -1)
    attn_out = jnp.dot(
        mixed, lax.all_gather(wo, "tile", axis=1, tiled=True), preferred_element_type=jnp.float32
    )
    hidden1 = hidden0 + gate_vec * attn_out
    final = layer_norm(hidden1).astype(jnp.bfloat16)
    eps_pred = jnp.dot(final, out_w, preferred_element_type=jnp.float32).astype(jnp.bfloat16)
    return eps_pred.reshape(count, tokens_tile, token_values)


def finish_kernel(scale_ref, left_ref, mid_ref, right_ref, w_ref, noise_ref, est_ref, next_ref):
    channels, pixels = est_ref.shape
    cols = (left_ref.shape[1] - pixels) // 2
    shifted = (left_ref, mid_ref, right_ref)
    blended = None
    for a in range(3):
        for b in range(3):
            window = shifted[b][:, a * cols : a * cols + pixels]
            term = jnp.dot(
                w_ref[3 * a + b], window,
                precision=lax.Precision.HIGHEST, preferred_element_type=jnp.float32,
            )
            blended = term if blended is None else blended + term
    raw = mid_ref[:, cols : cols + pixels]
    place = lax.broadcasted_iota(jnp.int32, (1, pixels), 1)
    row, col = place // cols, place % cols
    tile_px = pixels // cols
    seam = (row == 0) | (row == tile_px - 1) | (col % tile_px == 0) | (col % tile_px == tile_px - 1)
    estimate = jnp.where(seam, blended, raw)
    est_ref[...] = estimate
    next_ref[...] = scale_ref[0] * estimate + scale_ref[1] * noise_ref[...]


def seam_finish(raw, noise, conv_w, cos_prev, sin_prev):
    channels, rows, cols = raw.shape
    count = lax.axis_size("tile")
    forward = [(i, i + 1) for i in range(count - 1)]
    backward = [(target, source) for source, target in forward]
    low = lax.ppermute(raw[:, rows - 1 :], "tile", forward)
    high = lax.ppermute(raw[:, :1], "tile", backward)
    framed = jnp.pad(jnp.concatenate([low, raw, high], axis=1), ((0, 0), (0, 0), (1, 1)))
    shifted = [
        framed[:, :, b : b + cols].reshape(channels, (rows + 2) * cols) for b in range(3)
    ]
    scale = jnp.stack([cos_prev, sin_prev]).astype(jnp.float32)
    vmem = pl.BlockSpec(memory_space=pltpu.VMEM)
    flat = jax.ShapeDtypeStruct((channels, rows * cols), jnp.float32)
    estimate, next_latent = pl.pallas_call(
        finish_kernel,
        out_shape=(flat, flat),
        in_specs=[pl.BlockSpec(memory_space=pltpu.SMEM)] + [vmem] * 5,
        out_specs=(vmem, vmem),
    )(scale, *shifted, conv_w, noise.reshape(channels, rows * cols))
    return estimate.reshape(raw.shape), next_latent.reshape(raw.shape)


def on_device(
    latent,
    observed,
    noise,
    cloudy,
    timestep,
    pos_embed,
    embed_w,
    mod_w,
    wq,
    wk,
    wv,
    wo,
    q_gain,
    k_gain,
    out_w,
    conv_w,
):
    channels, band_rows, band_cols = latent.shape
    tile_side = band_rows // PATCH
    tiles_here = band_cols // band_rows
    width = embed_w.shape[1]
    step_now = timestep[0].astype(jnp.float32)
    cos_now, sin_now = plan(step_now)
    cos_prev, sin_prev = plan(step_now - STRIDE)
    time_code = time_features(step_now, mod_w.shape[0])
    local_mod = jnp.dot(time_code, mod_w, preferred_element_type=jnp.float32)
    modulation = lax.all_gather(local_mod, "tile", axis=1, tiled=True)
    shift_vec = modulation[:, :width]
    scale_vec = modulation[:, width : 2 * width]
    gate_vec = modulation[:, 2 * width :]
    tile_tokens = band_tiles(latent.astype(jnp.bfloat16), tile_side)
    order_in = jnp.cumsum(cloudy) - cloudy
    weights_all = (
        embed_w,
        pos_embed,
        shift_vec,
        scale_vec,
        gate_vec,
        wq,
        wk,
        wv,
        wo,
        q_gain,
        k_gain,
        out_w,
    )
    slot_ids = jnp.arange(MAXOWN, dtype=jnp.int32)
    slot_hit = (cloudy[None, :] == 1) & (order_in[None, :] == slot_ids[:, None])
    picked = jnp.sum(
        jnp.where(slot_hit, jnp.arange(tiles_here, dtype=jnp.int32)[None, :], 0), axis=1
    )
    chosen = jnp.take(tile_tokens, picked, axis=0)
    eps_chosen = denoise(chosen, *weights_all)
    eps_back = jnp.take(eps_chosen, jnp.minimum(order_in, MAXOWN - 1), axis=0)
    eps_tiles = jnp.where(cloudy[:, None, None] == 1, eps_back, jnp.zeros_like(eps_back))
    eps_latent = band_pixels(eps_tiles.astype(jnp.float32), tile_side, channels)
    cloud_cols = jnp.repeat(cloudy, band_rows) == 1
    raw_estimate = jnp.where(
        cloud_cols[None, None, :], (latent - sin_now * eps_latent) / cos_now, observed
    )
    estimate, next_latent = seam_finish(raw_estimate, noise, conv_w, cos_prev, sin_prev)
    return (estimate, next_latent)


def solution(mesh):
    placed = (
        P(None, ("grp", "tile"), None),
        P(None, ("grp", "tile"), None),
        P(None, ("grp", "tile"), None),
        P(("grp", "tile")),
        P("grp"),
        P(),
        P(),
        P(None, "tile"),
        P("tile", None),
        P("tile", None),
        P("tile", None),
        P(None, "tile"),
        P(),
        P(),
        P(),
        P(),
    )
    return jax.shard_map(
        on_device,
        mesh=mesh,
        in_specs=placed,
        out_specs=(P(None, ("grp", "tile"), None), P(None, ("grp", "tile"), None)),
        check_vma=False,
    )
```

```python
import math

import jax
import jax.numpy as jnp
from jax import lax
from jax.sharding import PartitionSpec as P

HD = 128
PATCH = 2
MAXOWN = 3
TSTEPS = 1000
STRIDE = 20


def padded_2(block, sides, width):
    for axis, dim in sides:
        count = lax.axis_size(axis)
        forward = [(i, i + 1) for i in range(count - 1)]
        backward = [(target, source) for source, target in forward]
        low = lax.ppermute(
            lax.slice_in_dim(block, block.shape[dim] - width, None, axis=dim), axis, forward
        )
        high = lax.ppermute(lax.slice_in_dim(block, 0, width, axis=dim), axis, backward)
        block = jnp.concatenate([low, block, high], axis=dim)
    return block


def plan(step):
    theta = (step / TSTEPS + 0.008) / 1.008 * (math.pi / 2)
    return (jnp.cos(theta), jnp.sin(theta))


def time_features(step, width):
    half = width // 2
    freqs = jnp.exp(-math.log(10000.0) * jnp.arange(half, dtype=jnp.float32) / half)
    angles = step * freqs
    code = jnp.concatenate([jnp.cos(angles), jnp.sin(angles)])[None, :]
    return jax.nn.silu(code).astype(jnp.bfloat16)


def layer_norm(values):
    center = values - jnp.mean(values, axis=-1, keepdims=True)
    spread = jnp.mean(center * center, axis=-1, keepdims=True)
    return center * lax.rsqrt(spread + 1e-06)


def head_norm(proj, gain, count, tokens_tile):
    shaped = proj.reshape(count, tokens_tile, -1, HD)
    scaled = shaped * lax.rsqrt(jnp.mean(shaped * shaped, axis=-1, keepdims=True) + 1e-06)
    return (scaled * gain).astype(jnp.bfloat16)


def band_tiles(band, tile_side):
    channels, band_rows, band_cols = band.shape
    tiles_here = band_cols // (tile_side * PATCH)
    shaped = band.reshape(channels, tile_side, PATCH, tiles_here, tile_side, PATCH)
    return jnp.transpose(shaped, (3, 1, 4, 2, 5, 0)).reshape(
        tiles_here, tile_side * tile_side, PATCH * PATCH * channels
    )


def band_pixels(tiled, tile_side, channels):
    tiles_here = tiled.shape[0]
    shaped = tiled.reshape(tiles_here, tile_side, tile_side, PATCH, PATCH, channels)
    return jnp.transpose(shaped, (5, 1, 3, 0, 2, 4)).reshape(
        channels, tile_side * PATCH, tiles_here * tile_side * PATCH
    )


def share_of_part(w_local):
    parts = lax.axis_size("grp")
    rows = w_local.shape[0] // parts
    return lax.dynamic_slice_in_dim(w_local, lax.axis_index("grp") * rows, rows, axis=0)


def add_rows(left, shard_rows):
    return jnp.dot(left, shard_rows, preferred_element_type=jnp.float32)


def denoise(
    chosen,
    embed_w,
    pos_embed,
    shift_vec,
    scale_vec,
    gate_vec,
    wq,
    wk,
    wv,
    wo,
    q_gain,
    k_gain,
    out_w,
):
    count, tokens_tile, token_values = chosen.shape
    row_count = count * tokens_tile
    flat = chosen.reshape(row_count, token_values)
    hidden0 = jnp.dot(flat, embed_w, preferred_element_type=jnp.float32).reshape(
        count, tokens_tile, -1
    )
    hidden0 = (hidden0 + pos_embed.astype(jnp.float32)[None]).reshape(row_count, -1)
    modulated = (layer_norm(hidden0) * (1.0 + scale_vec) + shift_vec).astype(jnp.bfloat16)

    def add_one(shard_rows):
        return add_rows(modulated, shard_rows)

    inner = wq.shape[1]
    qkv = lax.all_gather(share_of_part(jnp.concatenate([wq, wk, wv], axis=1)), ("tile", "grp"), axis=0, tiled=True)
    qkv_all = add_one(qkv)
    query_all = qkv_all[:, :inner]
    key_all = qkv_all[:, inner : 2 * inner]
    value_all = qkv_all[:, 2 * inner :]
    query_norm = head_norm(query_all, q_gain, count, tokens_tile)
    key_norm = head_norm(key_all, k_gain, count, tokens_tile)
    value_half = value_all.reshape(count, tokens_tile, -1, HD).astype(jnp.bfloat16)
    scores = jnp.einsum(
        "nqhd,nkhd->nhqk", query_norm, key_norm, preferred_element_type=jnp.float32
    ) * HD ** (-0.5)
    peak = jnp.max(scores, axis=-1, keepdims=True)
    expo = jnp.exp(scores - peak)
    probs = (expo / jnp.sum(expo, axis=-1, keepdims=True)).astype(jnp.bfloat16)
    mixed = jnp.einsum("nhqk,nkhd->nqhd", probs, value_half, preferred_element_type=jnp.float32)
    mixed = mixed.astype(jnp.bfloat16).reshape(row_count, -1)
    attn_out = jnp.dot(
        mixed, lax.all_gather(wo, "tile", axis=1, tiled=True), preferred_element_type=jnp.float32
    )
    hidden1 = hidden0 + gate_vec * attn_out
    final = layer_norm(hidden1).astype(jnp.bfloat16)
    eps_pred = jnp.dot(final, out_w, preferred_element_type=jnp.float32).astype(jnp.bfloat16)
    return eps_pred.reshape(count, tokens_tile, token_values)


def on_device(
    latent,
    observed,
    noise,
    cloudy,
    timestep,
    pos_embed,
    embed_w,
    mod_w,
    wq,
    wk,
    wv,
    wo,
    q_gain,
    k_gain,
    out_w,
    conv_w,
):
    channels, band_rows, band_cols = latent.shape
    tile_side = band_rows // PATCH
    tiles_here = band_cols // band_rows
    width = embed_w.shape[1]
    step_now = timestep[0].astype(jnp.float32)
    cos_now, sin_now = plan(step_now)
    cos_prev, sin_prev = plan(step_now - STRIDE)
    time_code = time_features(step_now, mod_w.shape[0])
    local_mod = jnp.dot(time_code, mod_w, preferred_element_type=jnp.float32)
    modulation = lax.all_gather(local_mod, "tile", axis=1, tiled=True)
    shift_vec = modulation[:, :width]
    scale_vec = modulation[:, width : 2 * width]
    gate_vec = modulation[:, 2 * width :]
    tile_tokens = band_tiles(latent.astype(jnp.bfloat16), tile_side)
    order_in = jnp.cumsum(cloudy) - cloudy
    weights_all = (
        embed_w,
        pos_embed,
        shift_vec,
        scale_vec,
        gate_vec,
        wq,
        wk,
        wv,
        wo,
        q_gain,
        k_gain,
        out_w,
    )
    slot_ids = jnp.arange(MAXOWN, dtype=jnp.int32)
    slot_hit = (cloudy[None, :] == 1) & (order_in[None, :] == slot_ids[:, None])
    picked = jnp.sum(
        jnp.where(slot_hit, jnp.arange(tiles_here, dtype=jnp.int32)[None, :], 0), axis=1
    )
    chosen = jnp.take(tile_tokens, picked, axis=0)
    eps_chosen = denoise(chosen, *weights_all)
    slot = jnp.minimum(order_in, MAXOWN - 1)[:, None, None]
    eps_back = eps_chosen[MAXOWN - 1][None]
    for index in range(MAXOWN - 2, -1, -1):
        eps_back = jnp.where(slot == index, eps_chosen[index][None], eps_back)
    eps_tiles = jnp.where(cloudy[:, None, None] == 1, eps_back, jnp.zeros_like(eps_back))
    eps_latent = band_pixels(eps_tiles.astype(jnp.float32), tile_side, channels)
    cloud_cols = jnp.repeat(cloudy, band_rows) == 1
    raw_estimate = jnp.where(
        cloud_cols[None, None, :], (latent - sin_now * eps_latent) / cos_now, observed
    )
    padded = padded_2(raw_estimate, (("tile", 1),), 1)
    padded = jnp.pad(padded, ((0, 0), (0, 0), (1, 1)))
    blended = jnp.zeros_like(raw_estimate)
    for row_shift in range(3):
        for col_shift in range(3):
            window = padded[:, row_shift : row_shift + band_rows, col_shift : col_shift + band_cols]
            blended = blended + jnp.einsum(
                "oc,chw->ohw",
                conv_w[3 * row_shift + col_shift],
                window,
                precision=lax.Precision.HIGHEST,
            )
    row_pos = jnp.arange(band_rows) % band_rows
    col_pos = jnp.arange(band_cols) % band_rows
    seam_mask = ((row_pos == 0) | (row_pos == band_rows - 1))[:, None] | (
        (col_pos == 0) | (col_pos == band_rows - 1)
    )[None, :]
    estimate = jnp.where(seam_mask[None], blended, raw_estimate)
    next_latent = cos_prev * estimate + sin_prev * noise
    return (estimate, next_latent)


def solution(mesh):
    placed = (
        P(None, ("grp", "tile"), None),
        P(None, ("grp", "tile"), None),
        P(None, ("grp", "tile"), None),
        P(("grp", "tile")),
        P("grp"),
        P(),
        P(),
        P(None, "tile"),
        P("tile", None),
        P("tile", None),
        P("tile", None),
        P(None, "tile"),
        P(),
        P(),
        P(),
        P(),
    )
    return jax.shard_map(
        on_device,
        mesh=mesh,
        in_specs=placed,
        out_specs=(P(None, ("grp", "tile"), None), P(None, ("grp", "tile"), None)),
        check_vma=False,
    )
```

```python
import math

import jax
import jax.numpy as jnp
from jax import lax
from jax.sharding import PartitionSpec as P

HD = 128
PATCH = 2
MAXOWN = 3
TSTEPS = 1000
STRIDE = 20


def padded_2(block, sides, width):
    for axis, dim in sides:
        count = lax.axis_size(axis)
        forward = [(i, i + 1) for i in range(count - 1)]
        backward = [(target, source) for source, target in forward]
        low = lax.ppermute(
            lax.slice_in_dim(block, block.shape[dim] - width, None, axis=dim), axis, forward
        )
        high = lax.ppermute(lax.slice_in_dim(block, 0, width, axis=dim), axis, backward)
        block = jnp.concatenate([low, block, high], axis=dim)
    return block


def plan(step):
    theta = (step / TSTEPS + 0.008) / 1.008 * (math.pi / 2)
    return (jnp.cos(theta), jnp.sin(theta))


def time_features(step, width):
    half = width // 2
    freqs = jnp.exp(-math.log(10000.0) * jnp.arange(half, dtype=jnp.float32) / half)
    angles = step * freqs
    code = jnp.concatenate([jnp.cos(angles), jnp.sin(angles)])[None, :]
    return jax.nn.silu(code).astype(jnp.bfloat16)


def layer_norm(values):
    center = values - jnp.mean(values, axis=-1, keepdims=True)
    spread = jnp.mean(center * center, axis=-1, keepdims=True)
    return center * lax.rsqrt(spread + 1e-06)


def head_norm(proj, gain, count, tokens_tile):
    shaped = proj.reshape(count, tokens_tile, -1, HD)
    scaled = shaped * lax.rsqrt(jnp.mean(shaped * shaped, axis=-1, keepdims=True) + 1e-06)
    return (scaled * gain).astype(jnp.bfloat16)


def band_tiles(band, tile_side):
    channels, band_rows, band_cols = band.shape
    tiles_here = band_cols // (tile_side * PATCH)
    shaped = band.reshape(channels, tile_side, PATCH, tiles_here, tile_side, PATCH)
    return jnp.transpose(shaped, (3, 1, 4, 2, 5, 0)).reshape(
        tiles_here, tile_side * tile_side, PATCH * PATCH * channels
    )


def band_pixels(tiled, tile_side, channels):
    tiles_here = tiled.shape[0]
    shaped = tiled.reshape(tiles_here, tile_side, tile_side, PATCH, PATCH, channels)
    return jnp.transpose(shaped, (5, 1, 3, 0, 2, 4)).reshape(
        channels, tile_side * PATCH, tiles_here * tile_side * PATCH
    )


def share_of_part(w_local):
    parts = lax.axis_size("grp")
    rows = w_local.shape[0] // parts
    return lax.dynamic_slice_in_dim(w_local, lax.axis_index("grp") * rows, rows, axis=0)


def add_rows(left, shard_rows):
    return jnp.dot(left, shard_rows, preferred_element_type=jnp.float32)


def denoise(
    chosen,
    embed_w,
    pos_embed,
    shift_vec,
    scale_vec,
    gate_vec,
    wq,
    wk,
    wv,
    wo,
    q_gain,
    k_gain,
    out_w,
):
    count, tokens_tile, token_values = chosen.shape
    row_count = count * tokens_tile
    flat = chosen.reshape(row_count, token_values)
    hidden0 = jnp.dot(flat, embed_w, preferred_element_type=jnp.float32).reshape(
        count, tokens_tile, -1
    )
    hidden0 = (hidden0 + pos_embed.astype(jnp.float32)[None]).reshape(row_count, -1)
    modulated = (layer_norm(hidden0) * (1.0 + scale_vec) + shift_vec).astype(jnp.bfloat16)

    def add_one(shard_rows):
        return add_rows(modulated, shard_rows)

    inner = wq.shape[1]
    qkv = lax.all_gather(share_of_part(jnp.concatenate([wq, wk, wv], axis=1)), ("tile", "grp"), axis=0, tiled=True)
    qkv_all = add_one(qkv)
    query_all = qkv_all[:, :inner]
    key_all = qkv_all[:, inner : 2 * inner]
    value_all = qkv_all[:, 2 * inner :]
    query_norm = head_norm(query_all, q_gain, count, tokens_tile)
    key_norm = head_norm(key_all, k_gain, count, tokens_tile)
    value_half = value_all.reshape(count, tokens_tile, -1, HD).astype(jnp.bfloat16)
    scores = jnp.einsum(
        "nqhd,nkhd->nhqk", query_norm, key_norm, preferred_element_type=jnp.float32
    ) * HD ** (-0.5)
    peak = jnp.max(scores, axis=-1, keepdims=True)
    expo = jnp.exp(scores - peak)
    probs = (expo / jnp.sum(expo, axis=-1, keepdims=True)).astype(jnp.bfloat16)
    mixed = jnp.einsum("nhqk,nkhd->nqhd", probs, value_half, preferred_element_type=jnp.float32)
    mixed = mixed.astype(jnp.bfloat16).reshape(row_count, -1)
    attn_out = jnp.dot(
        mixed, lax.all_gather(wo, "tile", axis=1, tiled=True), preferred_element_type=jnp.float32
    )
    hidden1 = hidden0 + gate_vec * attn_out
    final = layer_norm(hidden1).astype(jnp.bfloat16)
    eps_pred = jnp.dot(final, out_w, preferred_element_type=jnp.float32).astype(jnp.bfloat16)
    return eps_pred.reshape(count, tokens_tile, token_values)


def on_device(
    latent,
    observed,
    noise,
    cloudy,
    timestep,
    pos_embed,
    embed_w,
    mod_w,
    wq,
    wk,
    wv,
    wo,
    q_gain,
    k_gain,
    out_w,
    conv_w,
):
    channels, band_rows, band_cols = latent.shape
    tile_side = band_rows // PATCH
    tiles_here = band_cols // band_rows
    width = embed_w.shape[1]
    step_now = timestep[0].astype(jnp.float32)
    cos_now, sin_now = plan(step_now)
    cos_prev, sin_prev = plan(step_now - STRIDE)
    time_code = time_features(step_now, mod_w.shape[0])
    local_mod = jnp.dot(time_code, mod_w, preferred_element_type=jnp.float32)
    modulation = lax.all_gather(local_mod, "tile", axis=1, tiled=True)
    shift_vec = modulation[:, :width]
    scale_vec = modulation[:, width : 2 * width]
    gate_vec = modulation[:, 2 * width :]
    tile_tokens = band_tiles(latent.astype(jnp.bfloat16), tile_side)
    order_in = jnp.cumsum(cloudy) - cloudy
    weights_all = (
        embed_w,
        pos_embed,
        shift_vec,
        scale_vec,
        gate_vec,
        wq,
        wk,
        wv,
        wo,
        q_gain,
        k_gain,
        out_w,
    )
    slot_ids = jnp.arange(MAXOWN, dtype=jnp.int32)
    slot_hit = (cloudy[None, :] == 1) & (order_in[None, :] == slot_ids[:, None])
    picked = jnp.sum(
        jnp.where(slot_hit, jnp.arange(tiles_here, dtype=jnp.int32)[None, :], 0), axis=1
    )
    chosen = jnp.take(tile_tokens, picked, axis=0)
    eps_chosen = denoise(chosen, *weights_all)
    slot = jnp.minimum(order_in, MAXOWN - 1)
    eps_tiles = []
    for tile in range(tiles_here):
        tile_eps = eps_chosen[MAXOWN - 1]
        for index in range(MAXOWN - 2, -1, -1):
            tile_eps = jnp.where(slot[tile] == index, eps_chosen[index], tile_eps)
        eps_tiles.append(tile_eps)
    eps_latent = band_pixels(jnp.stack(eps_tiles).astype(jnp.float32), tile_side, channels)
    cloud_cols = jnp.repeat(cloudy, band_rows) == 1
    raw_estimate = jnp.where(
        cloud_cols[None, None, :], (latent - sin_now * eps_latent) / cos_now, observed
    )
    padded = padded_2(raw_estimate, (("tile", 1),), 1)
    padded = jnp.pad(padded, ((0, 0), (0, 0), (1, 1)))
    blended = jnp.zeros_like(raw_estimate)
    for row_shift in range(3):
        for col_shift in range(3):
            window = padded[:, row_shift : row_shift + band_rows, col_shift : col_shift + band_cols]
            blended = blended + jnp.einsum(
                "oc,chw->ohw",
                conv_w[3 * row_shift + col_shift],
                window,
                precision=lax.Precision.HIGHEST,
            )
    row_pos = jnp.arange(band_rows) % band_rows
    col_pos = jnp.arange(band_cols) % band_rows
    seam_mask = ((row_pos == 0) | (row_pos == band_rows - 1))[:, None] | (
        (col_pos == 0) | (col_pos == band_rows - 1)
    )[None, :]
    estimate = jnp.where(seam_mask[None], blended, raw_estimate)
    next_latent = cos_prev * estimate + sin_prev * noise
    return (estimate, next_latent)


def solution(mesh):
    placed = (
        P(None, ("grp", "tile"), None),
        P(None, ("grp", "tile"), None),
        P(None, ("grp", "tile"), None),
        P(("grp", "tile")),
        P("grp"),
        P(),
        P(),
        P(None, "tile"),
        P("tile", None),
        P("tile", None),
        P("tile", None),
        P(None, "tile"),
        P(),
        P(),
        P(),
        P(),
    )
    return jax.shard_map(
        on_device,
        mesh=mesh,
        in_specs=placed,
        out_specs=(P(None, ("grp", "tile"), None), P(None, ("grp", "tile"), None)),
        check_vma=False,
    )
```

```python
import math

import jax
import jax.numpy as jnp
from jax import lax
from jax.sharding import PartitionSpec as P

HD = 128
PATCH = 2
MAXOWN = 3
TSTEPS = 1000
STRIDE = 20


def padded_2(block, sides, width):
    for axis, dim in sides:
        count = lax.axis_size(axis)
        forward = [(i, i + 1) for i in range(count - 1)]
        backward = [(target, source) for source, target in forward]
        low = lax.ppermute(
            lax.slice_in_dim(block, block.shape[dim] - width, None, axis=dim), axis, forward
        )
        high = lax.ppermute(lax.slice_in_dim(block, 0, width, axis=dim), axis, backward)
        block = jnp.concatenate([low, block, high], axis=dim)
    return block


def plan(step):
    theta = (step / TSTEPS + 0.008) / 1.008 * (math.pi / 2)
    return (jnp.cos(theta), jnp.sin(theta))


def time_features(step, width):
    half = width // 2
    freqs = jnp.exp(-math.log(10000.0) * jnp.arange(half, dtype=jnp.float32) / half)
    angles = step * freqs
    code = jnp.concatenate([jnp.cos(angles), jnp.sin(angles)])[None, :]
    return jax.nn.silu(code).astype(jnp.bfloat16)


def layer_norm(values):
    center = values - jnp.mean(values, axis=-1, keepdims=True)
    spread = jnp.mean(center * center, axis=-1, keepdims=True)
    return center * lax.rsqrt(spread + 1e-06)


def head_norm(proj, gain, count, tokens_tile):
    shaped = proj.reshape(count, tokens_tile, -1, HD)
    scaled = shaped * lax.rsqrt(jnp.mean(shaped * shaped, axis=-1, keepdims=True) + 1e-06)
    return (scaled * gain).astype(jnp.bfloat16)


def band_tiles(band, tile_side):
    channels, band_rows, band_cols = band.shape
    tiles_here = band_cols // (tile_side * PATCH)
    shaped = band.reshape(channels, tile_side, PATCH, tiles_here, tile_side, PATCH)
    return jnp.transpose(shaped, (3, 1, 4, 2, 5, 0)).reshape(
        tiles_here, tile_side * tile_side, PATCH * PATCH * channels
    )


def band_pixels(tiled, tile_side, channels):
    tiles_here = tiled.shape[0]
    shaped = tiled.reshape(tiles_here, tile_side, tile_side, PATCH, PATCH, channels)
    return jnp.transpose(shaped, (5, 1, 3, 0, 2, 4)).reshape(
        channels, tile_side * PATCH, tiles_here * tile_side * PATCH
    )


def share_of_part(w_local):
    parts = lax.axis_size("grp")
    rows = w_local.shape[0] // parts
    return lax.dynamic_slice_in_dim(w_local, lax.axis_index("grp") * rows, rows, axis=0)


def add_rows(left, shard_rows):
    return jnp.dot(left, shard_rows, preferred_element_type=jnp.float32)


def denoise(
    chosen,
    embed_w,
    pos_embed,
    shift_vec,
    scale_vec,
    gate_vec,
    wq,
    wk,
    wv,
    wo,
    q_gain,
    k_gain,
    out_w,
):
    count, tokens_tile, token_values = chosen.shape
    row_count = count * tokens_tile
    flat = chosen.reshape(row_count, token_values)
    hidden0 = jnp.dot(flat, embed_w, preferred_element_type=jnp.float32).reshape(
        count, tokens_tile, -1
    )
    hidden0 = (hidden0 + pos_embed.astype(jnp.float32)[None]).reshape(row_count, -1)
    modulated = (layer_norm(hidden0) * (1.0 + scale_vec) + shift_vec).astype(jnp.bfloat16)

    def add_one(shard_rows):
        return add_rows(modulated, shard_rows)

    inner = wq.shape[1]
    qkv = lax.all_gather(share_of_part(jnp.concatenate([wq, wk, wv], axis=1)), ("tile", "grp"), axis=0, tiled=True)
    qkv_all = add_one(qkv)
    query_all = qkv_all[:, :inner]
    key_all = qkv_all[:, inner : 2 * inner]
    value_all = qkv_all[:, 2 * inner :]
    query_norm = head_norm(query_all, q_gain, count, tokens_tile)
    key_norm = head_norm(key_all, k_gain, count, tokens_tile)
    value_half = value_all.reshape(count, tokens_tile, -1, HD).astype(jnp.bfloat16)
    scores = jnp.einsum(
        "nqhd,nkhd->nhqk", query_norm, key_norm, preferred_element_type=jnp.float32
    ) * HD ** (-0.5)
    peak = jnp.max(scores, axis=-1, keepdims=True)
    expo = jnp.exp(scores - peak)
    probs = (expo / jnp.sum(expo, axis=-1, keepdims=True)).astype(jnp.bfloat16)
    mixed = jnp.einsum("nhqk,nkhd->nqhd", probs, value_half, preferred_element_type=jnp.float32)
    mixed = mixed.astype(jnp.bfloat16).reshape(row_count, -1)
    attn_out = jnp.dot(
        mixed, lax.all_gather(wo, "tile", axis=1, tiled=True), preferred_element_type=jnp.float32
    )
    hidden1 = hidden0 + gate_vec * attn_out
    final = layer_norm(hidden1).astype(jnp.bfloat16)
    eps_pred = jnp.dot(final, out_w, preferred_element_type=jnp.float32).astype(jnp.bfloat16)
    return eps_pred.reshape(count, tokens_tile, token_values)


def on_device(
    latent,
    observed,
    noise,
    cloudy,
    timestep,
    pos_embed,
    embed_w,
    mod_w,
    wq,
    wk,
    wv,
    wo,
    q_gain,
    k_gain,
    out_w,
    conv_w,
):
    channels, band_rows, band_cols = latent.shape
    tile_side = band_rows // PATCH
    tiles_here = band_cols // band_rows
    width = embed_w.shape[1]
    step_now = timestep[0].astype(jnp.float32)
    cos_now, sin_now = plan(step_now)
    cos_prev, sin_prev = plan(step_now - STRIDE)
    time_code = time_features(step_now, mod_w.shape[0])
    local_mod = jnp.dot(time_code, mod_w, preferred_element_type=jnp.float32)
    modulation = lax.all_gather(local_mod, "tile", axis=1, tiled=True)
    shift_vec = modulation[:, :width]
    scale_vec = modulation[:, width : 2 * width]
    gate_vec = modulation[:, 2 * width :]
    tile_tokens = band_tiles(latent.astype(jnp.bfloat16), tile_side)
    order_in = jnp.cumsum(cloudy) - cloudy
    weights_all = (
        embed_w,
        pos_embed,
        shift_vec,
        scale_vec,
        gate_vec,
        wq,
        wk,
        wv,
        wo,
        q_gain,
        k_gain,
        out_w,
    )
    slot_ids = jnp.arange(MAXOWN, dtype=jnp.int32)
    slot_hit = (cloudy[None, :] == 1) & (order_in[None, :] == slot_ids[:, None])
    picked = jnp.sum(
        jnp.where(slot_hit, jnp.arange(tiles_here, dtype=jnp.int32)[None, :], 0), axis=1
    )
    chosen = jnp.take(tile_tokens, picked, axis=0)
    eps_chosen = denoise(chosen, *weights_all)
    slot_px = band_pixels(eps_chosen.astype(jnp.float32), tile_side, channels)
    slot = jnp.minimum(order_in, MAXOWN - 1)
    tile_px = tile_side * PATCH
    blocks = [slot_px[:, :, index * tile_px : (index + 1) * tile_px] for index in range(MAXOWN)]
    columns = []
    for tile in range(tiles_here):
        block = blocks[MAXOWN - 1]
        for index in range(MAXOWN - 2, -1, -1):
            block = jnp.where(slot[tile] == index, blocks[index], block)
        columns.append(block)
    eps_latent = jnp.concatenate(columns, axis=2)
    cloud_cols = jnp.repeat(cloudy, band_rows) == 1
    raw_estimate = jnp.where(
        cloud_cols[None, None, :], (latent - sin_now * eps_latent) / cos_now, observed
    )
    padded = padded_2(raw_estimate, (("tile", 1),), 1)
    padded = jnp.pad(padded, ((0, 0), (0, 0), (1, 1)))
    blended = jnp.zeros_like(raw_estimate)
    for row_shift in range(3):
        for col_shift in range(3):
            window = padded[:, row_shift : row_shift + band_rows, col_shift : col_shift + band_cols]
            blended = blended + jnp.einsum(
                "oc,chw->ohw",
                conv_w[3 * row_shift + col_shift],
                window,
                precision=lax.Precision.HIGHEST,
            )
    row_pos = jnp.arange(band_rows) % band_rows
    col_pos = jnp.arange(band_cols) % band_rows
    seam_mask = ((row_pos == 0) | (row_pos == band_rows - 1))[:, None] | (
        (col_pos == 0) | (col_pos == band_rows - 1)
    )[None, :]
    estimate = jnp.where(seam_mask[None], blended, raw_estimate)
    next_latent = cos_prev * estimate + sin_prev * noise
    return (estimate, next_latent)


def solution(mesh):
    placed = (
        P(None, ("grp", "tile"), None),
        P(None, ("grp", "tile"), None),
        P(None, ("grp", "tile"), None),
        P(("grp", "tile")),
        P("grp"),
        P(),
        P(),
        P(None, "tile"),
        P("tile", None),
        P("tile", None),
        P("tile", None),
        P(None, "tile"),
        P(),
        P(),
        P(),
        P(),
    )
    return jax.shard_map(
        on_device,
        mesh=mesh,
        in_specs=placed,
        out_specs=(P(None, ("grp", "tile"), None), P(None, ("grp", "tile"), None)),
        check_vma=False,
    )
```
